256 devices in a mesh: tm: 4 (over x_lo, core), lat: 64 (over x_hi, z, y).
Axes of the slice: x: 4 (x_hi: 2, x_lo: 2; x = x_hi * 2 + x_lo), y: 4, z: 8, core: 2. Of those that a mesh axis runs over, the one named last changes fastest.
Arguments:
- field_in: float32 [8, 128, 128, 256], P('tm', 'lat'), may hold values from -6 to 6
- qkv_local: float32 [256, 768], replicated, may hold values from -0.5 to 0.5
- out_local: float32 [256, 256], replicated, may hold values from -0.5 to 0.5
- qkv_dilated: float32 [256, 768], replicated, may hold values from -0.5 to 0.5
- out_dilated: float32 [256, 256], replicated, may hold values from -0.5 to 0.5
- cotangent: float32 [8, 128, 128, 256], P('tm', 'lat'), may hold values from -6 to 6
Outputs:
- field_out: float32 [8, 128, 128, 256], P('tm', 'lat')
- field_grad: float32 [8, 128, 128, 256], P('tm', 'lat')
- grad_qkv_local: float32 [256, 768], replicated
- grad_out_local: float32 [256, 256], replicated
- grad_qkv_dilated: float32 [256, 768], replicated
- grad_out_dilated: float32 [256, 256], replicated
The draws below stay inside these ranges and needn't reach their ends.
All inputs are finite; a program needn't handle non-finite values.
Results may differ from the reference program's by a relative error of at most 0.0003.
Values sent between devices are 32-bit elements; how exact they have to be, the bound alone decides.
No kernel may reach another device: no remote copies, remote signals or barrier semaphores. Data moves between devices by JAX's collectives and lax.ppermute only.
A program may use at most 128 MiB of HBM per device.

```python
import math
from functools import partial
import jax
import jax.numpy as jnp
from jax import lax

C = 256
HEADS = 8
LAT_DEV = 2
W = 128
BT = 2
BH = 2
BWL = 16
BWD = 1
T_SIZE = 8
H = 128
N_LAT = 64


def level_of(own_key, extent, cuts, least, largest):
    factor_of, own = 1.0, jax.random.fold_in(own_key, 6)
    for dim, blocks in cuts:
        steps = jnp.exp(jax.random.uniform(jax.random.fold_in(own, dim), (blocks,), jnp.float32, least / len(cuts), largest / len(cuts)))
        factor_of = factor_of * jnp.repeat(steps, extent[dim] // blocks).reshape([-1 if axis == dim else 1 for axis in range(len(extent))])
    return factor_of


def gaussian(rng, shape, width, bound, shards=(), kind=jnp.bfloat16):
    level = level_of(rng, shape, shards, -0.22, 0.18) if shards else 1.0
    values = jax.random.normal(rng, shape, jnp.float32) * width * level
    return jnp.minimum(jnp.maximum(values, -bound), bound).astype(kind)


def setup_inputs(seed: int = 0) -> dict:
    splits = jax.random.split(jax.random.key(seed), 7)
    field_in = gaussian(splits[0], (T_SIZE, H, W, C), 1.0, 6.0, ((0, 4), (1, 64)), jnp.float32)
    qkv_local = gaussian(splits[1], (C, 3 * C), (C // 2) ** -0.5, 0.5, (), jnp.float32)
    out_local = gaussian(splits[2], (C, C), (C // 2) ** -0.5, 0.5, (), jnp.float32)
    qkv_dilated = gaussian(splits[3], (C, 3 * C), (C // 2) ** -0.5, 0.5, (), jnp.float32)
    out_dilated = gaussian(splits[4], (C, C), (C // 2) ** -0.5, 0.5, (), jnp.float32)
    cotangent = gaussian(splits[5], (T_SIZE, H, W, C), 1.0, 6.0, ((0, 4), (1, 64)), jnp.float32)
    return dict(field_in=field_in, qkv_local=qkv_local, out_local=out_local, qkv_dilated=qkv_dilated, out_dilated=out_dilated, cotangent=cotangent)


norm_eps = 1e-05

def normalize(values):
    center = values - lax.optimization_barrier(jnp.mean(values, axis=-1, keepdims=True))
    spread = lax.optimization_barrier(jnp.mean(center * center, axis=-1, keepdims=True))
    return center * lax.rsqrt(spread + norm_eps)

def project(values, weight):
    flat = values.reshape(-1, values.shape[-1])
    result = jnp.dot(flat, weight, precision=lax.Precision.HIGHEST, preferred_element_type=jnp.float32)
    return result.reshape(values.shape[:-1] + (weight.shape[1],))

def to_windows(tensor):
    steps_n, rows_n, lons_n, feats_n = tensor.shape
    shaped = tensor.reshape(steps_n // BT, BT, rows_n // BH, BH, lons_n // BWL, BWL, feats_n)
    shaped = shaped.transpose(0, 2, 4, 1, 3, 5, 6)
    return shaped.reshape(steps_n // BT, rows_n // BH * (lons_n // BWL), BT * BH * BWL, feats_n)

def from_windows(windows, steps_n, rows_n, lons_n):
    feats_n = windows.shape[-1]
    shaped = windows.reshape(steps_n // BT, rows_n // BH, lons_n // BWL, BT, BH, BWL, feats_n)
    shaped = shaped.transpose(0, 3, 1, 4, 2, 5, 6)
    return shaped.reshape(steps_n, rows_n, lons_n, feats_n)

def to_groups(tensor):
    steps_n, bands_n, rows_n, lons_n, feats_n = tensor.shape
    shaped = tensor.reshape(steps_n, bands_n, rows_n, lons_n // BWD, BWD, feats_n)
    shaped = shaped.transpose(0, 2, 3, 1, 4, 5)
    return shaped.reshape(steps_n, rows_n * (lons_n // BWD), bands_n * BWD, feats_n)

def from_groups(groups, bands_n, rows_n, lons_n):
    steps_n = groups.shape[0]
    feats_n = groups.shape[-1]
    shaped = groups.reshape(steps_n, rows_n, lons_n // BWD, bands_n, BWD, feats_n)
    shaped = shaped.transpose(0, 3, 1, 2, 4, 5)
    return shaped.reshape(steps_n, bands_n, rows_n, lons_n, feats_n)

def window_mask(steps_n, rows_n, lons_n, time_base, lat_base, total_time, total_lat):
    time_pos = time_base + jnp.arange(steps_n, dtype=jnp.int32)
    lat_pos = lat_base + jnp.arange(rows_n, dtype=jnp.int32)
    time_flag = (time_pos >= total_time - BT // 2).astype(jnp.int32)
    lat_flag = (lat_pos >= total_lat - BH // 2).astype(jnp.int32)
    labels = 2 * time_flag[:, None, None] + lat_flag[None, :, None] + jnp.zeros((1, 1, lons_n), jnp.int32)
    labelled = to_windows(labels[..., None])[..., 0]
    return labelled[..., :, None] == labelled[..., None, :]

def attend(packed, allowed):
    cells = packed.shape[1]
    channels = packed.shape[2] // 3
    head_dim = channels // HEADS
    pieces = packed.reshape(packed.shape[0], cells, 3, HEADS, head_dim)
    queries = pieces[:, :, 0]
    keys_part = pieces[:, :, 1]
    values_part = pieces[:, :, 2]
    scores = jnp.einsum('glhd,gmhd->ghlm', queries, keys_part, precision=lax.Precision.HIGHEST) * head_dim ** (-0.5)
    exponent = jnp.exp(scores)
    if allowed is not None:
        exponent = jnp.where(allowed[:, None, :, :], exponent, 0.0)
    shares = exponent / lax.optimization_barrier(jnp.sum(exponent, axis=-1, keepdims=True))
    blended = jnp.einsum('ghlm,gmhd->glhd', shares, values_part, precision=lax.Precision.HIGHEST)
    return blended.reshape(packed.shape[0], cells, channels)

def masked_block(pair):
    return attend(pair[0], pair[1])

def open_block(packed):
    return attend(packed, None)

def local_branch(shifted, weight_qkv, weight_out, allowed):
    moved = jnp.roll(shifted, -(BWL // 2), axis=2)
    mixed_qkv = project(normalize(moved), weight_qkv)
    windows = to_windows(mixed_qkv)
    attended = lax.map(jax.checkpoint(masked_block), (windows, allowed))
    back = from_windows(attended, shifted.shape[0], shifted.shape[1], shifted.shape[2])
    return jnp.roll(moved + project(back, weight_out), BWL // 2, axis=2)

def dilated_branch(banded, weight_qkv, weight_out):
    mixed_qkv = project(normalize(banded), weight_qkv)
    groups = to_groups(mixed_qkv)
    attended = lax.map(jax.checkpoint(open_block), groups)
    back = from_groups(attended, banded.shape[1], banded.shape[2], banded.shape[3])
    return project(back, weight_out)

def reference(field_in, qkv_local, out_local, qkv_dilated, out_dilated, cotangent):
    total_time, total_lat, total_lon, channels = field_in.shape
    allowed = window_mask(total_time, total_lat, total_lon, 0, 0, total_time, total_lat)
    local_fn = jax.checkpoint(partial(local_branch, allowed=allowed))
    dilated_fn = jax.checkpoint(dilated_branch)

    def forward(field, w_qs, w_os, w_qd, w_od):
        shifted = jnp.roll(field, (-(BT // 2), -(BH // 2)), axis=(0, 1))
        middle = jnp.roll(local_fn(shifted, w_qs, w_os), (BT // 2, BH // 2), axis=(0, 1))
        banded = middle.reshape(total_time, N_LAT, LAT_DEV, total_lon, channels)
        return middle + dilated_fn(banded, w_qd, w_od).reshape(middle.shape)
    field_out, pull = jax.vjp(forward, field_in, qkv_local, out_local, qkv_dilated, out_dilated)
    grads = pull(cotangent)
    factor = 1.0 / math.sqrt(total_time * total_lat * total_lon)
    return (field_out, grads[0], grads[1] * factor, grads[2] * factor, grads[3] * factor, grads[4] * factor)
```

```python
from functools import partial
import math

import jax
import jax.numpy as jnp
from jax import lax
from jax.sharding import PartitionSpec as P

HEADS = 8
BT = 2
BH = 2
BWL = 16
BWD = 1


norm_eps = 1e-05


def from_behind(shard, axis, by):
    size = lax.axis_size(axis)
    return lax.ppermute(shard, axis, [(i, (i + by) % size) for i in range(size)])


def normalize(values):
    center = values - jnp.mean(values, axis=-1, keepdims=True)
    spread = jnp.mean(center * center, axis=-1, keepdims=True)
    return center * lax.rsqrt(spread + norm_eps)


def project(values, weight):
    flat = values.reshape(-1, values.shape[-1])
    result = jnp.dot(
        flat, weight, precision=lax.Precision.HIGHEST, preferred_element_type=jnp.float32
    )
    return result.reshape(values.shape[:-1] + (weight.shape[1],))


def to_windows(tensor):
    steps_n, rows_n, lons_n, feats_n = tensor.shape
    shaped = tensor.reshape(steps_n // BT, BT, rows_n // BH, BH, lons_n // BWL, BWL, feats_n)
    shaped = shaped.transpose(0, 2, 4, 1, 3, 5, 6)
    return shaped.reshape(steps_n // BT, rows_n // BH * (lons_n // BWL), BT * BH * BWL, feats_n)


def from_windows(windows, steps_n, rows_n, lons_n):
    feats_n = windows.shape[-1]
    shaped = windows.reshape(steps_n // BT, rows_n // BH, lons_n // BWL, BT, BH, BWL, feats_n)
    shaped = shaped.transpose(0, 3, 1, 4, 2, 5, 6)
    return shaped.reshape(steps_n, rows_n, lons_n, feats_n)


def to_groups(tensor):
    steps_n, bands_n, rows_n, lons_n, feats_n = tensor.shape
    shaped = tensor.reshape(steps_n, bands_n, rows_n, lons_n // BWD, BWD, feats_n)
    shaped = shaped.transpose(0, 2, 3, 1, 4, 5)
    return shaped.reshape(steps_n, rows_n * (lons_n // BWD), bands_n * BWD, feats_n)


def from_groups(groups, bands_n, rows_n, lons_n):
    steps_n = groups.shape[0]
    feats_n = groups.shape[-1]
    shaped = groups.reshape(steps_n, rows_n, lons_n // BWD, bands_n, BWD, feats_n)
    shaped = shaped.transpose(0, 3, 1, 2, 4, 5)
    return shaped.reshape(steps_n, bands_n, rows_n, lons_n, feats_n)


def window_mask(steps_n, rows_n, lons_n, time_base, lat_base, total_time, total_lat):
    time_pos = time_base + jnp.arange(steps_n, dtype=jnp.int32)
    lat_pos = lat_base + jnp.arange(rows_n, dtype=jnp.int32)
    time_flag = (time_pos >= total_time - BT // 2).astype(jnp.int32)
    lat_flag = (lat_pos >= total_lat - BH // 2).astype(jnp.int32)
    labels = (
        2 * time_flag[:, None, None]
        + lat_flag[None, :, None]
        + jnp.zeros((1, 1, lons_n), jnp.int32)
    )
    labelled = to_windows(labels[..., None])[..., 0]
    return labelled[..., :, None] == labelled[..., None, :]


def attend(packed, allowed):
    cells = packed.shape[1]
    channels = packed.shape[2] // 3
    head_dim = channels // HEADS
    pieces = packed.reshape(packed.shape[0], cells, 3, HEADS, head_dim)
    queries = pieces[:, :, 0]
    keys_part = pieces[:, :, 1]
    values_part = pieces[:, :, 2]
    scores = jnp.einsum(
        "glhd,gmhd->ghlm", queries, keys_part, precision=lax.Precision.HIGHEST
    ) * head_dim ** (-0.5)
    exponent = jnp.exp(scores)
    if allowed is not None:
        exponent = jnp.where(allowed[:, None, :, :], exponent, 0.0)
    shares = exponent / jnp.sum(exponent, axis=-1, keepdims=True)
    blended = jnp.einsum("ghlm,gmhd->glhd", shares, values_part, precision=lax.Precision.HIGHEST)
    return blended.reshape(packed.shape[0], cells, channels)


def local_branch(shifted, weight_qkv, weight_out, allowed):
    moved = jnp.roll(shifted, -(BWL // 2), axis=2)
    mixed_qkv = project(normalize(moved), weight_qkv)
    windows = to_windows(mixed_qkv)
    cells = windows.shape[2]
    attended = attend(
        windows.reshape(-1, cells, windows.shape[3]), allowed.reshape(-1, cells, cells)
    )
    attended = attended.reshape(windows.shape[:3] + (shifted.shape[3],))
    back = from_windows(attended, shifted.shape[0], shifted.shape[1], shifted.shape[2])
    return jnp.roll(moved + project(back, weight_out), BWL // 2, axis=2)


def dilated_branch(banded, weight_qkv, weight_out):
    mixed_qkv = project(normalize(banded), weight_qkv)
    groups = to_groups(mixed_qkv)
    cells = groups.shape[2]
    attended = attend(groups.reshape(-1, cells, groups.shape[3]), None)
    attended = attended.reshape(groups.shape[:3] + (banded.shape[4],))
    back = from_groups(attended, banded.shape[1], banded.shape[2], banded.shape[3])
    return project(back, weight_out)


def butterfly_stages(axes):
    stages = []
    for axis in axes:
        size = lax.axis_size(axis)
        bits = size.bit_length() - 1
        if size != 1 << bits:
            return None
        stages += [(axis, bit) for bit in range(bits)]
    return stages


def swap_partner(value, axis, bit):
    size = lax.axis_size(axis)
    return lax.ppermute(value, axis, [(i, i ^ (1 << bit)) for i in range(size)])


def butterfly_sum(parts, axes):
    stages = butterfly_stages(axes)
    flat = jnp.concatenate([p.reshape(-1) for p in parts])
    if stages is None or flat.shape[0] % (1 << len(stages)):
        return lax.psum(parts, axes)
    for axis, bit in stages:
        upper = (lax.axis_index(axis) >> bit) & 1
        half = flat.shape[0] // 2
        low, high = flat[:half], flat[half:]
        sent = swap_partner(jnp.where(upper == 0, high, low), axis, bit)
        flat = jnp.where(upper == 0, low, high) + sent
    for axis, bit in reversed(stages):
        upper = (lax.axis_index(axis) >> bit) & 1
        got = swap_partner(flat, axis, bit)
        flat = jnp.where(
            upper == 0, jnp.concatenate([flat, got]), jnp.concatenate([got, flat])
        )
    out, start = [], 0
    for p in parts:
        out.append(flat[start:start + p.size].reshape(p.shape))
        start += p.size
    return tuple(out)


def advance_one(stacked):
    time_edge = BT // 2
    ahead_rows = from_behind(stacked[:, :time_edge], "tm", -1)
    moved = jnp.concatenate((stacked[:, time_edge:], ahead_rows), axis=1)
    lat_edge = BH // 2
    ahead_rows = from_behind(moved[:, :, :lat_edge], "lat", -1)
    return jnp.concatenate((moved[:, :, lat_edge:], ahead_rows), axis=2)


def retreat_one(stacked):
    time_edge = BT // 2
    behind_rows = from_behind(stacked[:, -time_edge:], "tm", 1)
    moved = jnp.concatenate((behind_rows, stacked[:, :-time_edge]), axis=1)
    lat_edge = BH // 2
    behind_rows = from_behind(moved[:, :, -lat_edge:], "lat", 1)
    return jnp.concatenate((behind_rows, moved[:, :, :-lat_edge]), axis=2)


def on_device(field_in, qkv_local, out_local, qkv_dilated, out_dilated, cotangent):
    steps_here, rows_here, lon_count, channels = field_in.shape
    total_time = steps_here * lax.axis_size("tm")
    total_lat = rows_here * lax.axis_size("lat")
    time_base = lax.axis_index("tm") * steps_here
    lat_base = lax.axis_index("lat") * rows_here
    mask_local = window_mask(
        steps_here, rows_here, lon_count, time_base, lat_base, total_time, total_lat
    )
    local_fn = partial(local_branch, allowed=mask_local)
    shifted = advance_one(field_in[None])[0]
    mid_local, pull_local = jax.vjp(local_fn, shifted, qkv_local, out_local)
    middle = retreat_one(mid_local[None])[0]
    banded = middle.reshape(steps_here, 1, rows_here, lon_count, channels)
    grad_banded = cotangent.reshape(steps_here, 1, rows_here, lon_count, channels)
    grouped = lax.all_to_all(banded, "lat", split_axis=3, concat_axis=1, tiled=True)
    group_out, pull_dilated = jax.vjp(dilated_branch, grouped, qkv_dilated, out_dilated)
    branch_out = lax.all_to_all(group_out, "lat", split_axis=1, concat_axis=3, tiled=True)
    grad_grouped = lax.all_to_all(grad_banded, "lat", split_axis=3, concat_axis=1, tiled=True)
    grad_group_in, grad_qkv_d, grad_out_d = pull_dilated(grad_grouped)
    grad_back = lax.all_to_all(grad_group_in, "lat", split_axis=1, concat_axis=3, tiled=True)
    total_mid = middle + branch_out.reshape(middle.shape)
    grad_middle = cotangent + grad_back.reshape(middle.shape)
    grad_shifted = advance_one(grad_middle[None])[0]
    grad_field_s, grad_qkv_s, grad_out_s = pull_local(grad_shifted)
    field_grad = retreat_one(grad_field_s[None])[0]
    factor = 1.0 / math.sqrt(total_time * total_lat * lon_count)
    summed = butterfly_sum(
        (grad_qkv_s * factor, grad_out_s * factor, grad_qkv_d * factor, grad_out_d * factor),
        ("tm", "lat"),
    )
    return (total_mid, field_grad, summed[0], summed[1], summed[2], summed[3])


def solution(mesh):
    return jax.shard_map(
        on_device,
        mesh=mesh,
        in_specs=(P("tm", "lat", None, None), P(), P(), P(), P(), P("tm", "lat", None, None)),
        out_specs=(P("tm", "lat", None, None), P("tm", "lat", None, None), P(), P(), P(), P()),
        check_vma=False,
    )
```

```python
from functools import partial
import math

import jax
import jax.numpy as jnp
from jax import lax
from jax.sharding import PartitionSpec as P

HEADS = 8
BT = 2
BH = 2
BWL = 16
BWD = 1


norm_eps = 1e-05


def from_behind(shard, axis, by):
    size = lax.axis_size(axis)
    return lax.ppermute(shard, axis, [(i, (i + by) % size) for i in range(size)])


def normalize(values):
    center = values - jnp.mean(values, axis=-1, keepdims=True)
    spread = jnp.mean(center * center, axis=-1, keepdims=True)
    return center * lax.rsqrt(spread + norm_eps)


def project(values, weight):
    flat = values.reshape(-1, values.shape[-1])
    result = jnp.dot(
        flat, weight, precision=lax.Precision.HIGHEST, preferred_element_type=jnp.float32
    )
    return result.reshape(values.shape[:-1] + (weight.shape[1],))


def to_windows(tensor):
    steps_n, rows_n, lons_n, feats_n = tensor.shape
    shaped = tensor.reshape(steps_n // BT, BT, rows_n // BH, BH, lons_n // BWL, BWL, feats_n)
    shaped = shaped.transpose(0, 2, 4, 1, 3, 5, 6)
    return shaped.reshape(steps_n // BT, rows_n // BH * (lons_n // BWL), BT * BH * BWL, feats_n)


def from_windows(windows, steps_n, rows_n, lons_n):
    feats_n = windows.shape[-1]
    shaped = windows.reshape(steps_n // BT, rows_n // BH, lons_n // BWL, BT, BH, BWL, feats_n)
    shaped = shaped.transpose(0, 3, 1, 4, 2, 5, 6)
    return shaped.reshape(steps_n, rows_n, lons_n, feats_n)


def to_groups(tensor):
    steps_n, bands_n, rows_n, lons_n, feats_n = tensor.shape
    shaped = tensor.reshape(steps_n, bands_n, rows_n, lons_n // BWD, BWD, feats_n)
    shaped = shaped.transpose(0, 2, 3, 1, 4, 5)
    return shaped.reshape(steps_n, rows_n * (lons_n // BWD), bands_n * BWD, feats_n)


def from_groups(groups, bands_n, rows_n, lons_n):
    steps_n = groups.shape[0]
    feats_n = groups.shape[-1]
    shaped = groups.reshape(steps_n, rows_n, lons_n // BWD, bands_n, BWD, feats_n)
    shaped = shaped.transpose(0, 3, 1, 2, 4, 5)
    return shaped.reshape(steps_n, bands_n, rows_n, lons_n, feats_n)


def window_mask(steps_n, rows_n, lons_n, time_base, lat_base, total_time, total_lat):
    time_pos = time_base + jnp.arange(steps_n, dtype=jnp.int32)
    lat_pos = lat_base + jnp.arange(rows_n, dtype=jnp.int32)
    time_flag = (time_pos >= total_time - BT // 2).astype(jnp.int32)
    lat_flag = (lat_pos >= total_lat - BH // 2).astype(jnp.int32)
    labels = (
        2 * time_flag[:, None, None]
        + lat_flag[None, :, None]
        + jnp.zeros((1, 1, lons_n), jnp.int32)
    )
    labelled = to_windows(labels[..., None])[..., 0]
    return labelled[..., :, None] == labelled[..., None, :]


def attend(packed, allowed):
    cells = packed.shape[1]
    channels = packed.shape[2] // 3
    head_dim = channels // HEADS
    pieces = packed.reshape(packed.shape[0], cells, 3, HEADS, head_dim)
    queries = pieces[:, :, 0]
    keys_part = pieces[:, :, 1]
    values_part = pieces[:, :, 2]
    scores = jnp.einsum(
        "glhd,gmhd->ghlm", queries, keys_part, precision=lax.Precision.HIGHEST
    ) * head_dim ** (-0.5)
    exponent = jnp.exp(scores)
    if allowed is not None:
        exponent = jnp.where(allowed[:, None, :, :], exponent, 0.0)
    shares = exponent / jnp.sum(exponent, axis=-1, keepdims=True)
    blended = jnp.einsum("ghlm,gmhd->glhd", shares, values_part, precision=lax.Precision.HIGHEST)
    return blended.reshape(packed.shape[0], cells, channels)


def dilated_branch(banded, weight_qkv, weight_out):
    mixed_qkv = project(normalize(banded), weight_qkv)
    groups = to_groups(mixed_qkv)
    cells = groups.shape[2]
    attended = attend(groups.reshape(-1, cells, groups.shape[3]), None)
    attended = attended.reshape(groups.shape[:3] + (banded.shape[4],))
    back = from_groups(attended, banded.shape[1], banded.shape[2], banded.shape[3])
    return project(back, weight_out)


def butterfly_stages(axes):
    stages = []
    for axis in axes:
        size = lax.axis_size(axis)
        bits = size.bit_length() - 1
        if size != 1 << bits:
            return None
        stages += [(axis, bit) for bit in range(bits)]
    return stages


def swap_partner(value, axis, bit):
    size = lax.axis_size(axis)
    return lax.ppermute(value, axis, [(i, i ^ (1 << bit)) for i in range(size)])


def butterfly_sum(parts, axes):
    stages = butterfly_stages(axes)
    flat = jnp.concatenate([p.reshape(-1) for p in parts])
    if stages is None or flat.shape[0] % (1 << len(stages)):
        return lax.psum(parts, axes)
    for axis, bit in stages:
        upper = (lax.axis_index(axis) >> bit) & 1
        half = flat.shape[0] // 2
        low, high = flat[:half], flat[half:]
        sent = swap_partner(jnp.where(upper == 0, high, low), axis, bit)
        flat = jnp.where(upper == 0, low, high) + sent
    for axis, bit in reversed(stages):
        upper = (lax.axis_index(axis) >> bit) & 1
        got = swap_partner(flat, axis, bit)
        flat = jnp.where(
            upper == 0, jnp.concatenate([flat, got]), jnp.concatenate([got, flat])
        )
    out, start = [], 0
    for p in parts:
        out.append(flat[start:start + p.size].reshape(p.shape))
        start += p.size
    return tuple(out)


def shift_grid(stacked, step):
    time_edge = BT // 2
    lat_edge = BH // 2
    tm_size = lax.axis_size("tm")
    lat_size = lax.axis_size("lat")
    by = -step
    if step == 1:
        own = stacked[:, time_edge:, lat_edge:]
        lat_part = stacked[:, time_edge:, :lat_edge]
        tm_part = stacked[:, :time_edge, lat_edge:]
        corner = stacked[:, :time_edge, :lat_edge]
    else:
        own = stacked[:, :-time_edge, :-lat_edge]
        lat_part = stacked[:, :-time_edge, -lat_edge:]
        tm_part = stacked[:, -time_edge:, :-lat_edge]
        corner = stacked[:, -time_edge:, -lat_edge:]
    lat_part = from_behind(lat_part, "lat", by)
    tm_part = from_behind(tm_part, "tm", by)
    pairs = [
        (a * lat_size + b, ((a + by) % tm_size) * lat_size + (b + by) % lat_size)
        for a in range(tm_size)
        for b in range(lat_size)
    ]
    corner = lax.ppermute(corner, ("tm", "lat"), pairs)
    if step == 1:
        top = jnp.concatenate((own, lat_part), axis=2)
        bottom = jnp.concatenate((tm_part, corner), axis=2)
    else:
        top = jnp.concatenate((corner, tm_part), axis=2)
        bottom = jnp.concatenate((lat_part, own), axis=2)
    return jnp.concatenate((top, bottom), axis=1)


def local_shifted(moved, weight_qkv, weight_out, allowed):
    mixed_qkv = project(normalize(moved), weight_qkv)
    windows = to_windows(mixed_qkv)
    cells = windows.shape[2]
    attended = attend(
        windows.reshape(-1, cells, windows.shape[3]), allowed.reshape(-1, cells, cells)
    )
    attended = attended.reshape(windows.shape[:3] + (moved.shape[3],))
    back = from_windows(attended, moved.shape[0], moved.shape[1], moved.shape[2])
    return moved + project(back, weight_out)


def on_device(field_in, qkv_local, out_local, qkv_dilated, out_dilated, cotangent):
    steps_here, rows_here, lon_count, channels = field_in.shape
    total_time = steps_here * lax.axis_size("tm")
    total_lat = rows_here * lax.axis_size("lat")
    time_base = lax.axis_index("tm") * steps_here
    lat_base = lax.axis_index("lat") * rows_here
    mask_local = window_mask(
        steps_here, rows_here, lon_count, time_base, lat_base, total_time, total_lat
    )
    local_fn = partial(local_shifted, allowed=mask_local)
    pair = shift_grid(jnp.stack((field_in, cotangent)), 1)
    pair = jnp.roll(pair, -(BWL // 2), axis=3)
    moved, grad_moved = pair[0], pair[1]
    middle, pull_local = jax.vjp(local_fn, moved, qkv_local, out_local)
    banded = middle.reshape(steps_here, 1, rows_here, lon_count, channels)
    grad_banded = grad_moved.reshape(steps_here, 1, rows_here, lon_count, channels)
    grad_grouped = lax.all_to_all(grad_banded, "lat", split_axis=3, concat_axis=1, tiled=True)
    grouped = lax.all_to_all(banded, "lat", split_axis=3, concat_axis=1, tiled=True)
    group_out, pull_dilated = jax.vjp(dilated_branch, grouped, qkv_dilated, out_dilated)
    branch_out = lax.all_to_all(group_out, "lat", split_axis=1, concat_axis=3, tiled=True)
    total_mid = middle + branch_out.reshape(middle.shape)
    field_out = shift_grid(jnp.roll(total_mid, BWL // 2, axis=2)[None], -1)[0]
    grad_group_in, grad_qkv_d, grad_out_d = pull_dilated(grad_grouped)
    factor = 1.0 / math.sqrt(total_time * total_lat * lon_count)
    summed_d = butterfly_sum((grad_qkv_d * factor, grad_out_d * factor), ("tm", "lat"))
    grad_back = lax.all_to_all(grad_group_in, "lat", split_axis=1, concat_axis=3, tiled=True)
    grad_middle = grad_moved + grad_back.reshape(middle.shape)
    grad_field_s, grad_qkv_s, grad_out_s = pull_local(grad_middle)
    field_grad = shift_grid(jnp.roll(grad_field_s, BWL // 2, axis=2)[None], -1)[0]
    summed_s = butterfly_sum((grad_qkv_s * factor, grad_out_s * factor), ("tm", "lat"))
    return (field_out, field_grad, summed_s[0], summed_s[1], summed_d[0], summed_d[1])


def solution(mesh):
    return jax.shard_map(
        on_device,
        mesh=mesh,
        in_specs=(P("tm", "lat", None, None), P(), P(), P(), P(), P("tm", "lat", None, None)),
        out_specs=(P("tm", "lat", None, None), P("tm", "lat", None, None), P(), P(), P(), P()),
        check_vma=False,
    )
```

```python
from functools import partial
import math

import jax
import jax.numpy as jnp
from jax import lax
from jax.sharding import PartitionSpec as P

HEADS = 8
BT = 2
BH = 2
BWL = 16
BWD = 1


norm_eps = 1e-05


def from_behind(shard, axis, by):
    size = lax.axis_size(axis)
    return lax.ppermute(shard, axis, [(i, (i + by) % size) for i in range(size)])


def normalize(values):
    center = values - jnp.mean(values, axis=-1, keepdims=True)
    spread = jnp.mean(center * center, axis=-1, keepdims=True)
    return center * lax.rsqrt(spread + norm_eps)


def project(values, weight):
    flat = values.reshape(-1, values.shape[-1])
    result = jnp.dot(
        flat, weight, precision=lax.Precision.HIGHEST, preferred_element_type=jnp.float32
    )
    return result.reshape(values.shape[:-1] + (weight.shape[1],))


def to_windows(tensor):
    steps_n, rows_n, lons_n, feats_n = tensor.shape
    shaped = tensor.reshape(steps_n // BT, BT, rows_n // BH, BH, lons_n // BWL, BWL, feats_n)
    shaped = shaped.transpose(0, 2, 4, 1, 3, 5, 6)
    return shaped.reshape(steps_n // BT, rows_n // BH * (lons_n // BWL), BT * BH * BWL, feats_n)


def from_windows(windows, steps_n, rows_n, lons_n):
    feats_n = windows.shape[-1]
    shaped = windows.reshape(steps_n // BT, rows_n // BH, lons_n // BWL, BT, BH, BWL, feats_n)
    shaped = shaped.transpose(0, 3, 1, 4, 2, 5, 6)
    return shaped.reshape(steps_n, rows_n, lons_n, feats_n)


def to_groups(tensor):
    steps_n, bands_n, rows_n, lons_n, feats_n = tensor.shape
    shaped = tensor.reshape(steps_n, bands_n, rows_n, lons_n // BWD, BWD, feats_n)
    shaped = shaped.transpose(0, 2, 3, 1, 4, 5)
    return shaped.reshape(steps_n, rows_n * (lons_n // BWD), bands_n * BWD, feats_n)


def from_groups(groups, bands_n, rows_n, lons_n):
    steps_n = groups.shape[0]
    feats_n = groups.shape[-1]
    shaped = groups.reshape(steps_n, rows_n, lons_n // BWD, bands_n, BWD, feats_n)
    shaped = shaped.transpose(0, 3, 1, 2, 4, 5)
    return shaped.reshape(steps_n, bands_n, rows_n, lons_n, feats_n)


def window_mask(steps_n, rows_n, lons_n, time_base, lat_base, total_time, total_lat):
    time_pos = time_base + jnp.arange(steps_n, dtype=jnp.int32)
    lat_pos = lat_base + jnp.arange(rows_n, dtype=jnp.int32)
    time_flag = (time_pos >= total_time - BT // 2).astype(jnp.int32)
    lat_flag = (lat_pos >= total_lat - BH // 2).astype(jnp.int32)
    labels = (
        2 * time_flag[:, None, None]
        + lat_flag[None, :, None]
        + jnp.zeros((1, 1, lons_n), jnp.int32)
    )
    labelled = to_windows(labels[..., None])[..., 0]
    return labelled[..., :, None] == labelled[..., None, :]


def attend(packed, allowed):
    cells = packed.shape[1]
    channels = packed.shape[2] // 3
    head_dim = channels // HEADS
    pieces = packed.reshape(packed.shape[0], cells, 3, HEADS, head_dim)
    queries = pieces[:, :, 0]
    keys_part = pieces[:, :, 1]
    values_part = pieces[:, :, 2]
    scores = jnp.einsum(
        "glhd,gmhd->ghlm", queries, keys_part, precision=lax.Precision.HIGHEST
    ) * head_dim ** (-0.5)
    exponent = jnp.exp(scores)
    if allowed is not None:
        exponent = jnp.where(allowed[:, None, :, :], exponent, 0.0)
    shares = exponent / jnp.sum(exponent, axis=-1, keepdims=True)
    blended = jnp.einsum("ghlm,gmhd->glhd", shares, values_part, precision=lax.Precision.HIGHEST)
    return blended.reshape(packed.shape[0], cells, channels)


def dilated_branch(banded, weight_qkv, weight_out):
    mixed_qkv = project(normalize(banded), weight_qkv)
    groups = to_groups(mixed_qkv)
    cells = groups.shape[2]
    attended = attend(groups.reshape(-1, cells, groups.shape[3]), None)
    attended = attended.reshape(groups.shape[:3] + (banded.shape[4],))
    back = from_groups(attended, banded.shape[1], banded.shape[2], banded.shape[3])
    return project(back, weight_out)


def butterfly_stages(axes):
    stages = []
    for axis in axes:
        size = lax.axis_size(axis)
        bits = size.bit_length() - 1
        if size != 1 << bits:
            return None
        stages += [(axis, bit) for bit in range(bits)]
    return stages


def swap_partner(value, axis, bit):
    size = lax.axis_size(axis)
    return lax.ppermute(value, axis, [(i, i ^ (1 << bit)) for i in range(size)])


def butterfly_sum(parts, axes):
    stages = butterfly_stages(axes)
    flat = jnp.concatenate([p.reshape(-1) for p in parts])
    if stages is None or flat.shape[0] % (1 << len(stages)):
        return lax.psum(parts, axes)
    for axis, bit in stages:
        upper = (lax.axis_index(axis) >> bit) & 1
        half = flat.shape[0] // 2
        low, high = flat[:half], flat[half:]
        sent = swap_partner(jnp.where(upper == 0, high, low), axis, bit)
        flat = jnp.where(upper == 0, low, high) + sent
    for axis, bit in reversed(stages):
        upper = (lax.axis_index(axis) >> bit) & 1
        got = swap_partner(flat, axis, bit)
        flat = jnp.where(
            upper == 0, jnp.concatenate([flat, got]), jnp.concatenate([got, flat])
        )
    out, start = [], 0
    for p in parts:
        out.append(flat[start:start + p.size].reshape(p.shape))
        start += p.size
    return tuple(out)


def shift_grid(stacked, step):
    time_edge = BT // 2
    lat_edge = BH // 2
    tm_size = lax.axis_size("tm")
    lat_size = lax.axis_size("lat")
    by = -step
    if step == 1:
        own = stacked[:, time_edge:, lat_edge:]
        lat_part = stacked[:, time_edge:, :lat_edge]
        tm_part = stacked[:, :time_edge, lat_edge:]
        corner = stacked[:, :time_edge, :lat_edge]
    else:
        own = stacked[:, :-time_edge, :-lat_edge]
        lat_part = stacked[:, :-time_edge, -lat_edge:]
        tm_part = stacked[:, -time_edge:, :-lat_edge]
        corner = stacked[:, -time_edge:, -lat_edge:]
    lat_part = from_behind(lat_part, "lat", by)
    tm_part = from_behind(tm_part, "tm", by)
    pairs = [
        (a * lat_size + b, ((a + by) % tm_size) * lat_size + (b + by) % lat_size)
        for a in range(tm_size)
        for b in range(lat_size)
    ]
    corner = lax.ppermute(corner, ("tm", "lat"), pairs)
    if step == 1:
        top = jnp.concatenate((own, lat_part), axis=2)
        bottom = jnp.concatenate((tm_part, corner), axis=2)
    else:
        top = jnp.concatenate((corner, tm_part), axis=2)
        bottom = jnp.concatenate((lat_part, own), axis=2)
    return jnp.concatenate((top, bottom), axis=1)


def local_shifted(moved, weight_qkv, weight_out, allowed):
    mixed_qkv = project(normalize(moved), weight_qkv)
    windows = to_windows(mixed_qkv)
    cells = windows.shape[2]
    attended = attend(
        windows.reshape(-1, cells, windows.shape[3]), allowed.reshape(-1, cells, cells)
    )
    attended = attended.reshape(windows.shape[:3] + (moved.shape[3],))
    back = from_windows(attended, moved.shape[0], moved.shape[1], moved.shape[2])
    return moved + project(back, weight_out)


def on_device(field_in, qkv_local, out_local, qkv_dilated, out_dilated, cotangent):
    steps_here, rows_here, lon_count, channels = field_in.shape
    total_time = steps_here * lax.axis_size("tm")
    total_lat = rows_here * lax.axis_size("lat")
    time_base = lax.axis_index("tm") * steps_here
    lat_base = lax.axis_index("lat") * rows_here
    mask_local = window_mask(
        steps_here, rows_here, lon_count, time_base, lat_base, total_time, total_lat
    )
    local_fn = partial(local_shifted, allowed=mask_local)
    pair = shift_grid(jnp.stack((field_in, cotangent)), 1)
    pair = jnp.roll(pair, -(BWL // 2), axis=3)
    moved, grad_moved = pair[0], pair[1]
    middle, pull_local = jax.vjp(local_fn, moved, qkv_local, out_local)
    banded = middle.reshape(steps_here, 1, rows_here, lon_count, channels)
    grad_banded = grad_moved.reshape(steps_here, 1, rows_here, lon_count, channels)
    grad_grouped = lax.all_to_all(grad_banded, "lat", split_axis=3, concat_axis=1, tiled=True)
    grouped = lax.all_to_all(banded, "lat", split_axis=3, concat_axis=1, tiled=True)
    group_out, pull_dilated = jax.vjp(dilated_branch, grouped, qkv_dilated, out_dilated)
    branch_out = lax.all_to_all(group_out, "lat", split_axis=1, concat_axis=3, tiled=True)
    total_mid = middle + branch_out.reshape(middle.shape)
    field_out = shift_grid(jnp.roll(total_mid, BWL // 2, axis=2)[None], -1)[0]
    grad_group_in, grad_qkv_d, grad_out_d = pull_dilated(grad_grouped)
    grad_back = lax.all_to_all(grad_group_in, "lat", split_axis=1, concat_axis=3, tiled=True)
    grad_middle = grad_moved + grad_back.reshape(middle.shape)
    grad_field_s, grad_qkv_s, grad_out_s = pull_local(grad_middle)
    field_grad = shift_grid(jnp.roll(grad_field_s, BWL // 2, axis=2)[None], -1)[0]
    factor = 1.0 / math.sqrt(total_time * total_lat * lon_count)
    summed = butterfly_sum(
        (grad_qkv_s * factor, grad_out_s * factor, grad_qkv_d * factor, grad_out_d * factor),
        ("tm", "lat"),
    )
    return (field_out, field_grad, summed[0], summed[1], summed[2], summed[3])


def solution(mesh):
    return jax.shard_map(
        on_device,
        mesh=mesh,
        in_specs=(P("tm", "lat", None, None), P(), P(), P(), P(), P("tm", "lat", None, None)),
        out_specs=(P("tm", "lat", None, None), P("tm", "lat", None, None), P(), P(), P(), P()),
        check_vma=False,
    )
```

```python
from functools import partial
import math

import jax
import jax.numpy as jnp
from jax import lax
from jax.sharding import PartitionSpec as P

HEADS = 8
BT = 2
BH = 2
BWL = 16
BWD = 1


norm_eps = 1e-05


def from_behind(shard, axis, by):
    size = lax.axis_size(axis)
    return lax.ppermute(shard, axis, [(i, (i + by) % size) for i in range(size)])


def normalize(values):
    center = values - jnp.mean(values, axis=-1, keepdims=True)
    spread = jnp.mean(center * center, axis=-1, keepdims=True)
    return center * lax.rsqrt(spread + norm_eps)


def project(values, weight):
    flat = values.reshape(-1, values.shape[-1])
    result = jnp.dot(
        flat, weight, precision=lax.Precision.HIGHEST, preferred_element_type=jnp.float32
    )
    return result.reshape(values.shape[:-1] + (weight.shape[1],))


def to_windows(tensor):
    steps_n, rows_n, lons_n, feats_n = tensor.shape
    shaped = tensor.reshape(steps_n // BT, BT, rows_n // BH, BH, lons_n // BWL, BWL, feats_n)
    shaped = shaped.transpose(0, 2, 4, 1, 3, 5, 6)
    return shaped.reshape(steps_n // BT, rows_n // BH * (lons_n // BWL), BT * BH * BWL, feats_n)


def from_windows(windows, steps_n, rows_n, lons_n):
    feats_n = windows.shape[-1]
    shaped = windows.reshape(steps_n // BT, rows_n // BH, lons_n // BWL, BT, BH, BWL, feats_n)
    shaped = shaped.transpose(0, 3, 1, 4, 2, 5, 6)
    return shaped.reshape(steps_n, rows_n, lons_n, feats_n)


def to_groups(tensor):
    steps_n, bands_n, rows_n, lons_n, feats_n = tensor.shape
    shaped = tensor.reshape(steps_n, bands_n, rows_n, lons_n // BWD, BWD, feats_n)
    shaped = shaped.transpose(0, 2, 3, 1, 4, 5)
    return shaped.reshape(steps_n, rows_n * (lons_n // BWD), bands_n * BWD, feats_n)


def from_groups(groups, bands_n, rows_n, lons_n):
    steps_n = groups.shape[0]
    feats_n = groups.shape[-1]
    shaped = groups.reshape(steps_n, rows_n, lons_n // BWD, bands_n, BWD, feats_n)
    shaped = shaped.transpose(0, 3, 1, 2, 4, 5)
    return shaped.reshape(steps_n, bands_n, rows_n, lons_n, feats_n)


def window_mask(steps_n, rows_n, lons_n, time_base, lat_base, total_time, total_lat):
    time_pos = time_base + jnp.arange(steps_n, dtype=jnp.int32)
    lat_pos = lat_base + jnp.arange(rows_n, dtype=jnp.int32)
    time_flag = (time_pos >= total_time - BT // 2).astype(jnp.int32)
    lat_flag = (lat_pos >= total_lat - BH // 2).astype(jnp.int32)
    labels = (
        2 * time_flag[:, None, None]
        + lat_flag[None, :, None]
        + jnp.zeros((1, 1, lons_n), jnp.int32)
    )
    labelled = to_windows(labels[..., None])[..., 0]
    return labelled[..., :, None] == labelled[..., None, :]


def attend(packed, allowed):
    cells = packed.shape[1]
    channels = packed.shape[2] // 3
    head_dim = channels // HEADS
    pieces = packed.reshape(packed.shape[0], cells, 3, HEADS, head_dim)
    queries = pieces[:, :, 0]
    keys_part = pieces[:, :, 1]
    values_part = pieces[:, :, 2]
    scores = jnp.einsum(
        "glhd,gmhd->ghlm", queries, keys_part, precision=lax.Precision.HIGHEST
    ) * head_dim ** (-0.5)
    exponent = jnp.exp(scores)
    if allowed is not None:
        exponent = jnp.where(allowed[:, None, :, :], exponent, 0.0)
    shares = exponent / jnp.sum(exponent, axis=-1, keepdims=True)
    blended = jnp.einsum("ghlm,gmhd->glhd", shares, values_part, precision=lax.Precision.HIGHEST)
    return blended.reshape(packed.shape[0], cells, channels)


def dilated_branch(banded, weight_qkv, weight_out):
    mixed_qkv = project(normalize(banded), weight_qkv)
    groups = to_groups(mixed_qkv)
    cells = groups.shape[2]
    attended = attend(groups.reshape(-1, cells, groups.shape[3]), None)
    attended = attended.reshape(groups.shape[:3] + (banded.shape[4],))
    back = from_groups(attended, banded.shape[1], banded.shape[2], banded.shape[3])
    return project(back, weight_out)


def butterfly_stages(axes):
    stages = []
    for axis in axes:
        size = lax.axis_size(axis)
        bits = size.bit_length() - 1
        if size != 1 << bits:
            return None
        stages += [(axis, bit) for bit in range(bits)]
    return stages


def swap_partner(value, axis, bit):
    size = lax.axis_size(axis)
    return lax.ppermute(value, axis, [(i, i ^ (1 << bit)) for i in range(size)])


def butterfly_sum(parts, axes, side, side_stage):
    stages = butterfly_stages(axes)
    flat = jnp.concatenate([p.reshape(-1) for p in parts])
    if stages is None or flat.shape[0] % (1 << len(stages)):
        return lax.psum(parts, axes) + (side(),)
    side_value = side()
    for index, (axis, bit) in enumerate(stages):
        if index == side_stage:
            side_value, flat = lax.optimization_barrier((side_value, flat))
        upper = (lax.axis_index(axis) >> bit) & 1
        half = flat.shape[0] // 2
        low, high = flat[:half], flat[half:]
        sent = swap_partner(jnp.where(upper == 0, high, low), axis, bit)
        flat = jnp.where(upper == 0, low, high) + sent
    for axis, bit in reversed(stages):
        upper = (lax.axis_index(axis) >> bit) & 1
        got = swap_partner(flat, axis, bit)
        flat = jnp.where(
            upper == 0, jnp.concatenate([flat, got]), jnp.concatenate([got, flat])
        )
    out, start = [], 0
    for p in parts:
        out.append(flat[start:start + p.size].reshape(p.shape))
        start += p.size
    return tuple(out) + (side_value,)


def shift_grid(stacked, step):
    time_edge = BT // 2
    lat_edge = BH // 2
    tm_size = lax.axis_size("tm")
    lat_size = lax.axis_size("lat")
    by = -step
    if step == 1:
        own = stacked[:, time_edge:, lat_edge:]
        lat_part = stacked[:, time_edge:, :lat_edge]
        tm_part = stacked[:, :time_edge, lat_edge:]
        corner = stacked[:, :time_edge, :lat_edge]
    else:
        own = stacked[:, :-time_edge, :-lat_edge]
        lat_part = stacked[:, :-time_edge, -lat_edge:]
        tm_part = stacked[:, -time_edge:, :-lat_edge]
        corner = stacked[:, -time_edge:, -lat_edge:]
    lat_part = from_behind(lat_part, "lat", by)
    tm_part = from_behind(tm_part, "tm", by)
    pairs = [
        (a * lat_size + b, ((a + by) % tm_size) * lat_size + (b + by) % lat_size)
        for a in range(tm_size)
        for b in range(lat_size)
    ]
    corner = lax.ppermute(corner, ("tm", "lat"), pairs)
    if step == 1:
        top = jnp.concatenate((own, lat_part), axis=2)
        bottom = jnp.concatenate((tm_part, corner), axis=2)
    else:
        top = jnp.concatenate((corner, tm_part), axis=2)
        bottom = jnp.concatenate((lat_part, own), axis=2)
    return jnp.concatenate((top, bottom), axis=1)


def local_shifted(moved, weight_qkv, weight_out, allowed):
    mixed_qkv = project(normalize(moved), weight_qkv)
    windows = to_windows(mixed_qkv)
    cells = windows.shape[2]
    attended = attend(
        windows.reshape(-1, cells, windows.shape[3]), allowed.reshape(-1, cells, cells)
    )
    attended = attended.reshape(windows.shape[:3] + (moved.shape[3],))
    back = from_windows(attended, moved.shape[0], moved.shape[1], moved.shape[2])
    return moved + project(back, weight_out)


def on_device(field_in, qkv_local, out_local, qkv_dilated, out_dilated, cotangent):
    steps_here, rows_here, lon_count, channels = field_in.shape
    total_time = steps_here * lax.axis_size("tm")
    total_lat = rows_here * lax.axis_size("lat")
    time_base = lax.axis_index("tm") * steps_here
    lat_base = lax.axis_index("lat") * rows_here
    mask_local = window_mask(
        steps_here, rows_here, lon_count, time_base, lat_base, total_time, total_lat
    )
    local_fn = partial(local_shifted, allowed=mask_local)
    pair = shift_grid(jnp.stack((field_in, cotangent)), 1)
    pair = jnp.roll(pair, -(BWL // 2), axis=3)
    moved, grad_moved = pair[0], pair[1]
    middle, pull_local = jax.vjp(local_fn, moved, qkv_local, out_local)
    banded = middle.reshape(steps_here, 1, rows_here, lon_count, channels)
    grad_banded = grad_moved.reshape(steps_here, 1, rows_here, lon_count, channels)
    grad_grouped = lax.all_to_all(grad_banded, "lat", split_axis=3, concat_axis=1, tiled=True)
    grouped = lax.all_to_all(banded, "lat", split_axis=3, concat_axis=1, tiled=True)
    group_out, pull_dilated = jax.vjp(dilated_branch, grouped, qkv_dilated, out_dilated)
    grad_group_in, grad_qkv_d, grad_out_d = pull_dilated(grad_grouped)
    both_back = lax.all_to_all(
        jnp.stack((group_out, grad_group_in)), "lat", split_axis=2, concat_axis=4, tiled=True
    )
    total_mid = middle + both_back[0].reshape(middle.shape)
    grad_middle = grad_moved + both_back[1].reshape(middle.shape)
    grad_field_s, grad_qkv_s, grad_out_s = pull_local(grad_middle)
    factor = 1.0 / math.sqrt(total_time * total_lat * lon_count)
    parts = (grad_qkv_s * factor, grad_out_s * factor, grad_qkv_d * factor, grad_out_d * factor)
    results = jnp.roll(jnp.stack((total_mid, grad_field_s)), BWL // 2, axis=3)
    summed = butterfly_sum(parts, ("tm", "lat"), lambda: shift_grid(results, -1), 2)
    field_out, field_grad = summed[4][0], summed[4][1]
    return (field_out, field_grad, summed[0], summed[1], summed[2], summed[3])


def solution(mesh):
    return jax.shard_map(
        on_device,
        mesh=mesh,
        in_specs=(P("tm", "lat", None, None), P(), P(), P(), P(), P("tm", "lat", None, None)),
        out_specs=(P("tm", "lat", None, None), P("tm", "lat", None, None), P(), P(), P(), P()),
        check_vma=False,
    )
```

```python
from functools import partial
import math

import jax
import jax.numpy as jnp
from jax import lax
from jax.sharding import PartitionSpec as P

HEADS = 8
BT = 2
BH = 2
BWL = 16
BWD = 1


norm_eps = 1e-05


def from_behind(shard, axis, by):
    size = lax.axis_size(axis)
    return lax.ppermute(shard, axis, [(i, (i + by) % size) for i in range(size)])


def normalize(values):
    center = values - jnp.mean(values, axis=-1, keepdims=True)
    spread = jnp.mean(center * center, axis=-1, keepdims=True)
    return center * lax.rsqrt(spread + norm_eps)


def project(values, weight):
    flat = values.reshape(-1, values.shape[-1])
    result = jnp.dot(
        flat, weight, precision=lax.Precision.HIGHEST, preferred_element_type=jnp.float32
    )
    return result.reshape(values.shape[:-1] + (weight.shape[1],))


def to_windows(tensor):
    steps_n, rows_n, lons_n, feats_n = tensor.shape
    shaped = tensor.reshape(steps_n // BT, BT, rows_n // BH, BH, lons_n // BWL, BWL, feats_n)
    shaped = shaped.transpose(0, 2, 4, 1, 3, 5, 6)
    return shaped.reshape(steps_n // BT, rows_n // BH * (lons_n // BWL), BT * BH * BWL, feats_n)


def from_windows(windows, steps_n, rows_n, lons_n):
    feats_n = windows.shape[-1]
    shaped = windows.reshape(steps_n // BT, rows_n // BH, lons_n // BWL, BT, BH, BWL, feats_n)
    shaped = shaped.transpose(0, 3, 1, 4, 2, 5, 6)
    return shaped.reshape(steps_n, rows_n, lons_n, feats_n)


def to_groups(tensor):
    steps_n, bands_n, rows_n, lons_n, feats_n = tensor.shape
    shaped = tensor.reshape(steps_n, bands_n, rows_n, lons_n // BWD, BWD, feats_n)
    shaped = shaped.transpose(0, 2, 3, 1, 4, 5)
    return shaped.reshape(steps_n, rows_n * (lons_n // BWD), bands_n * BWD, feats_n)


def from_groups(groups, bands_n, rows_n, lons_n):
    steps_n = groups.shape[0]
    feats_n = groups.shape[-1]
    shaped = groups.reshape(steps_n, rows_n, lons_n // BWD, bands_n, BWD, feats_n)
    shaped = shaped.transpose(0, 3, 1, 2, 4, 5)
    return shaped.reshape(steps_n, bands_n, rows_n, lons_n, feats_n)


def window_mask(steps_n, rows_n, lons_n, time_base, lat_base, total_time, total_lat):
    time_pos = time_base + jnp.arange(steps_n, dtype=jnp.int32)
    lat_pos = lat_base + jnp.arange(rows_n, dtype=jnp.int32)
    time_flag = (time_pos >= total_time - BT // 2).astype(jnp.int32)
    lat_flag = (lat_pos >= total_lat - BH // 2).astype(jnp.int32)
    labels = (
        2 * time_flag[:, None, None]
        + lat_flag[None, :, None]
        + jnp.zeros((1, 1, lons_n), jnp.int32)
    )
    labelled = to_windows(labels[..., None])[..., 0]
    return labelled[..., :, None] == labelled[..., None, :]


def attend(packed, allowed):
    cells = packed.shape[1]
    channels = packed.shape[2] // 3
    head_dim = channels // HEADS
    queries = packed[..., :channels]
    keys_part = packed[..., channels:2 * channels]
    values_part = packed[..., 2 * channels:]
    head_of = (jnp.arange(channels) // head_dim)[:, None] == jnp.arange(HEADS)[None, :]
    head_of = head_of.astype(packed.dtype)
    spread_keys = jnp.swapaxes(keys_part, 1, 2)[:, :, None, :] * head_of[None, :, :, None]
    scores = jnp.einsum(
        "glc,gchm->glhm", queries, spread_keys, precision=lax.Precision.HIGHEST
    ) * head_dim ** (-0.5)
    exponent = jnp.exp(scores)
    if allowed is not None:
        exponent = jnp.where(allowed[:, :, None, :], exponent, 0.0)
    shares = exponent / jnp.sum(exponent, axis=-1, keepdims=True)
    spread_values = values_part[:, None, :, :] * jnp.transpose(head_of)[None, :, None, :]
    return jnp.einsum(
        "glhm,ghmc->glc", shares, spread_values, precision=lax.Precision.HIGHEST
    )


def dilated_branch(banded, weight_qkv, weight_out):
    mixed_qkv = project(normalize(banded), weight_qkv)
    groups = to_groups(mixed_qkv)
    cells = groups.shape[2]
    attended = attend(groups.reshape(-1, cells, groups.shape[3]), None)
    attended = attended.reshape(groups.shape[:3] + (banded.shape[4],))
    back = from_groups(attended, banded.shape[1], banded.shape[2], banded.shape[3])
    return project(back, weight_out)


def butterfly_stages(axes):
    stages = []
    for axis in axes:
        size = lax.axis_size(axis)
        bits = size.bit_length() - 1
        if size != 1 << bits:
            return None
        stages += [(axis, bit) for bit in range(bits)]
    return stages


def swap_partner(value, axis, bit):
    size = lax.axis_size(axis)
    return lax.ppermute(value, axis, [(i, i ^ (1 << bit)) for i in range(size)])


def butterfly_sum(parts, axes, side, side_stage):
    stages = butterfly_stages(axes)
    flat = jnp.concatenate([p.reshape(-1) for p in parts])
    if stages is None or flat.shape[0] % (1 << len(stages)):
        return lax.psum(parts, axes) + (side(),)
    side_value = side()
    for index, (axis, bit) in enumerate(stages):
        if index == side_stage:
            side_value, flat = lax.optimization_barrier((side_value, flat))
        upper = (lax.axis_index(axis) >> bit) & 1
        half = flat.shape[0] // 2
        low, high = flat[:half], flat[half:]
        sent = swap_partner(jnp.where(upper == 0, high, low), axis, bit)
        flat = jnp.where(upper == 0, low, high) + sent
    for axis, bit in reversed(stages):
        upper = (lax.axis_index(axis) >> bit) & 1
        got = swap_partner(flat, axis, bit)
        flat = jnp.where(
            upper == 0, jnp.concatenate([flat, got]), jnp.concatenate([got, flat])
        )
    out, start = [], 0
    for p in parts:
        out.append(flat[start:start + p.size].reshape(p.shape))
        start += p.size
    return tuple(out) + (side_value,)


def shift_grid(stacked, step):
    time_edge = BT // 2
    lat_edge = BH // 2
    tm_size = lax.axis_size("tm")
    lat_size = lax.axis_size("lat")
    by = -step
    if step == 1:
        own = stacked[:, time_edge:, lat_edge:]
        lat_part = stacked[:, time_edge:, :lat_edge]
        tm_part = stacked[:, :time_edge, lat_edge:]
        corner = stacked[:, :time_edge, :lat_edge]
    else:
        own = stacked[:, :-time_edge, :-lat_edge]
        lat_part = stacked[:, :-time_edge, -lat_edge:]
        tm_part = stacked[:, -time_edge:, :-lat_edge]
        corner = stacked[:, -time_edge:, -lat_edge:]
    lat_part = from_behind(lat_part, "lat", by)
    tm_part = from_behind(tm_part, "tm", by)
    pairs = [
        (a * lat_size + b, ((a + by) % tm_size) * lat_size + (b + by) % lat_size)
        for a in range(tm_size)
        for b in range(lat_size)
    ]
    corner = lax.ppermute(corner, ("tm", "lat"), pairs)
    if step == 1:
        top = jnp.concatenate((own, lat_part), axis=2)
        bottom = jnp.concatenate((tm_part, corner), axis=2)
    else:
        top = jnp.concatenate((corner, tm_part), axis=2)
        bottom = jnp.concatenate((lat_part, own), axis=2)
    return jnp.concatenate((top, bottom), axis=1)


def local_shifted(moved, weight_qkv, weight_out, allowed):
    mixed_qkv = project(normalize(moved), weight_qkv)
    windows = to_windows(mixed_qkv)
    cells = windows.shape[2]
    attended = attend(
        windows.reshape(-1, cells, windows.shape[3]), allowed.reshape(-1, cells, cells)
    )
    attended = attended.reshape(windows.shape[:3] + (moved.shape[3],))
    back = from_windows(attended, moved.shape[0], moved.shape[1], moved.shape[2])
    return moved + project(back, weight_out)


def on_device(field_in, qkv_local, out_local, qkv_dilated, out_dilated, cotangent):
    steps_here, rows_here, lon_count, channels = field_in.shape
    total_time = steps_here * lax.axis_size("tm")
    total_lat = rows_here * lax.axis_size("lat")
    time_base = lax.axis_index("tm") * steps_here
    lat_base = lax.axis_index("lat") * rows_here
    mask_local = window_mask(
        steps_here, rows_here, lon_count, time_base, lat_base, total_time, total_lat
    )
    local_fn = partial(local_shifted, allowed=mask_local)
    pair = shift_grid(jnp.stack((field_in, cotangent)), 1)
    pair = jnp.roll(pair, -(BWL // 2), axis=3)
    moved, grad_moved = pair[0], pair[1]
    middle, pull_local = jax.vjp(local_fn, moved, qkv_local, out_local)
    banded = middle.reshape(steps_here, 1, rows_here, lon_count, channels)
    grad_banded = grad_moved.reshape(steps_here, 1, rows_here, lon_count, channels)
    grad_grouped = lax.all_to_all(grad_banded, "lat", split_axis=3, concat_axis=1, tiled=True)
    grouped = lax.all_to_all(banded, "lat", split_axis=3, concat_axis=1, tiled=True)
    group_out, pull_dilated = jax.vjp(dilated_branch, grouped, qkv_dilated, out_dilated)
    grad_group_in, grad_qkv_d, grad_out_d = pull_dilated(grad_grouped)
    both_back = lax.all_to_all(
        jnp.stack((group_out, grad_group_in)), "lat", split_axis=2, concat_axis=4, tiled=True
    )
    total_mid = middle + both_back[0].reshape(middle.shape)
    grad_middle = grad_moved + both_back[1].reshape(middle.shape)
    grad_field_s, grad_qkv_s, grad_out_s = pull_local(grad_middle)
    factor = 1.0 / math.sqrt(total_time * total_lat * lon_count)
    parts = (grad_qkv_s * factor, grad_out_s * factor, grad_qkv_d * factor, grad_out_d * factor)
    results = jnp.roll(jnp.stack((total_mid, grad_field_s)), BWL // 2, axis=3)
    summed = butterfly_sum(parts, ("tm", "lat"), lambda: shift_grid(results, -1), 2)
    field_out, field_grad = summed[4][0], summed[4][1]
    return (field_out, field_grad, summed[0], summed[1], summed[2], summed[3])


def solution(mesh):
    return jax.shard_map(
        on_device,
        mesh=mesh,
        in_specs=(P("tm", "lat", None, None), P(), P(), P(), P(), P("tm", "lat", None, None)),
        out_specs=(P("tm", "lat", None, None), P("tm", "lat", None, None), P(), P(), P(), P()),
        check_vma=False,
    )
```

```python
from functools import partial
import math

import jax
import jax.numpy as jnp
from jax import lax
from jax.sharding import PartitionSpec as P

HEADS = 8
BT = 2
BH = 2
BWL = 16
BWD = 1


norm_eps = 1e-05


def from_behind(shard, axis, by):
    size = lax.axis_size(axis)
    return lax.ppermute(shard, axis, [(i, (i + by) % size) for i in range(size)])


def normalize(values):
    center = values - jnp.mean(values, axis=-1, keepdims=True)
    spread = jnp.mean(center * center, axis=-1, keepdims=True)
    return center * lax.rsqrt(spread + norm_eps)


def project(values, weight):
    flat = values.reshape(-1, values.shape[-1])
    result = jnp.dot(
        flat, weight, precision=lax.Precision.HIGHEST, preferred_element_type=jnp.float32
    )
    return result.reshape(values.shape[:-1] + (weight.shape[1],))


def to_windows(tensor):
    steps_n, rows_n, lons_n, feats_n = tensor.shape
    shaped = tensor.reshape(steps_n // BT, BT, rows_n // BH, BH, lons_n // BWL, BWL, feats_n)
    shaped = shaped.transpose(0, 2, 4, 1, 3, 5, 6)
    return shaped.reshape(steps_n // BT, rows_n // BH * (lons_n // BWL), BT * BH * BWL, feats_n)


def from_windows(windows, steps_n, rows_n, lons_n):
    feats_n = windows.shape[-1]
    shaped = windows.reshape(steps_n // BT, rows_n // BH, lons_n // BWL, BT, BH, BWL, feats_n)
    shaped = shaped.transpose(0, 3, 1, 4, 2, 5, 6)
    return shaped.reshape(steps_n, rows_n, lons_n, feats_n)


def to_groups(tensor):
    steps_n, bands_n, rows_n, lons_n, feats_n = tensor.shape
    shaped = tensor.reshape(steps_n, bands_n, rows_n, lons_n // BWD, BWD, feats_n)
    shaped = shaped.transpose(0, 2, 3, 1, 4, 5)
    return shaped.reshape(steps_n, rows_n * (lons_n // BWD), bands_n * BWD, feats_n)


def from_groups(groups, bands_n, rows_n, lons_n):
    steps_n = groups.shape[0]
    feats_n = groups.shape[-1]
    shaped = groups.reshape(steps_n, rows_n, lons_n // BWD, bands_n, BWD, feats_n)
    shaped = shaped.transpose(0, 3, 1, 2, 4, 5)
    return shaped.reshape(steps_n, bands_n, rows_n, lons_n, feats_n)


def window_mask(steps_n, rows_n, lons_n, time_base, lat_base, total_time, total_lat):
    time_pos = time_base + jnp.arange(steps_n, dtype=jnp.int32)
    lat_pos = lat_base + jnp.arange(rows_n, dtype=jnp.int32)
    time_flag = (time_pos >= total_time - BT // 2).astype(jnp.int32)
    lat_flag = (lat_pos >= total_lat - BH // 2).astype(jnp.int32)
    labels = (
        2 * time_flag[:, None, None]
        + lat_flag[None, :, None]
        + jnp.zeros((1, 1, lons_n), jnp.int32)
    )
    labelled = to_windows(labels[..., None])[..., 0]
    return labelled[..., :, None] == labelled[..., None, :]


def attend(packed, allowed):
    cells = packed.shape[1]
    channels = packed.shape[2] // 3
    head_dim = channels // HEADS
    queries = packed[..., :channels]
    keys_part = packed[..., channels:2 * channels]
    values_part = packed[..., 2 * channels:]
    head_of = (jnp.arange(channels) // head_dim)[:, None] == jnp.arange(HEADS)[None, :]
    head_of = head_of.astype(packed.dtype)
    spread_keys = jnp.swapaxes(keys_part, 1, 2)[:, :, None, :] * head_of[None, :, :, None]
    scores = jnp.einsum(
        "glc,gchm->glhm", queries, spread_keys, precision=lax.Precision.HIGHEST
    ) * head_dim ** (-0.5)
    exponent = jnp.exp(scores)
    if allowed is not None:
        exponent = jnp.where(allowed[:, :, None, :], exponent, 0.0)
    shares = exponent / jnp.sum(exponent, axis=-1, keepdims=True)
    spread_values = values_part[:, None, :, :] * jnp.transpose(head_of)[None, :, None, :]
    return jnp.einsum(
        "glhm,ghmc->glc", shares, spread_values, precision=lax.Precision.HIGHEST
    )


def dilated_branch(banded, weight_qkv, weight_out):
    mixed_qkv = project(normalize(banded), weight_qkv)
    groups = to_groups(mixed_qkv)
    cells = groups.shape[2]
    attended = attend(groups.reshape(-1, cells, groups.shape[3]), None)
    attended = attended.reshape(groups.shape[:3] + (banded.shape[4],))
    back = from_groups(attended, banded.shape[1], banded.shape[2], banded.shape[3])
    return project(back, weight_out)


def butterfly_stages(axes):
    stages = []
    for axis in axes:
        size = lax.axis_size(axis)
        bits = size.bit_length() - 1
        if size != 1 << bits:
            return None
        stages += [(axis, bit) for bit in range(bits)]
    return stages


def swap_partner(value, axis, bit):
    size = lax.axis_size(axis)
    return lax.ppermute(value, axis, [(i, i ^ (1 << bit)) for i in range(size)])


def butterfly_sum(parts, axes, side, side_stage, halvings=4):
    stages = butterfly_stages(axes)
    joined = jnp.concatenate(parts, axis=1)
    width = joined.shape[1]
    if stages is None or width % (128 << min(halvings, len(stages))):
        return lax.psum(parts, axes) + (side(),)
    halved = stages[:halvings]
    side_value = side()
    for index, (axis, bit) in enumerate(stages):
        if index == side_stage:
            side_value, joined = lax.optimization_barrier((side_value, joined))
        if index < len(halved):
            upper = (lax.axis_index(axis) >> bit) & 1
            half = joined.shape[1] // 2
            kept = lax.dynamic_slice_in_dim(joined, upper * half, half, axis=1)
            sent = lax.dynamic_slice_in_dim(joined, (1 - upper) * half, half, axis=1)
            joined = kept + swap_partner(sent, axis, bit)
        else:
            joined = joined + swap_partner(joined, axis, bit)
    for axis, bit in reversed(halved):
        upper = (lax.axis_index(axis) >> bit) & 1
        got = swap_partner(joined, axis, bit)
        joined = jnp.where(
            upper == 0,
            jnp.concatenate([joined, got], axis=1),
            jnp.concatenate([got, joined], axis=1),
        )
    out, start = [], 0
    for p in parts:
        out.append(joined[:, start:start + p.shape[1]])
        start += p.shape[1]
    return tuple(out) + (side_value,)


def shift_grid(stacked, step):
    time_edge = BT // 2
    lat_edge = BH // 2
    tm_size = lax.axis_size("tm")
    lat_size = lax.axis_size("lat")
    by = -step
    if step == 1:
        own = stacked[:, time_edge:, lat_edge:]
        lat_part = stacked[:, time_edge:, :lat_edge]
        tm_part = stacked[:, :time_edge, lat_edge:]
        corner = stacked[:, :time_edge, :lat_edge]
    else:
        own = stacked[:, :-time_edge, :-lat_edge]
        lat_part = stacked[:, :-time_edge, -lat_edge:]
        tm_part = stacked[:, -time_edge:, :-lat_edge]
        corner = stacked[:, -time_edge:, -lat_edge:]
    lat_part = from_behind(lat_part, "lat", by)
    tm_part = from_behind(tm_part, "tm", by)
    pairs = [
        (a * lat_size + b, ((a + by) % tm_size) * lat_size + (b + by) % lat_size)
        for a in range(tm_size)
        for b in range(lat_size)
    ]
    corner = lax.ppermute(corner, ("tm", "lat"), pairs)
    if step == 1:
        top = jnp.concatenate((own, lat_part), axis=2)
        bottom = jnp.concatenate((tm_part, corner), axis=2)
    else:
        top = jnp.concatenate((corner, tm_part), axis=2)
        bottom = jnp.concatenate((lat_part, own), axis=2)
    return jnp.concatenate((top, bottom), axis=1)


def local_shifted(moved, weight_qkv, weight_out, allowed):
    mixed_qkv = project(normalize(moved), weight_qkv)
    windows = to_windows(mixed_qkv)
    cells = windows.shape[2]
    attended = attend(
        windows.reshape(-1, cells, windows.shape[3]), allowed.reshape(-1, cells, cells)
    )
    attended = attended.reshape(windows.shape[:3] + (moved.shape[3],))
    back = from_windows(attended, moved.shape[0], moved.shape[1], moved.shape[2])
    return moved + project(back, weight_out)


def on_device(field_in, qkv_local, out_local, qkv_dilated, out_dilated, cotangent):
    steps_here, rows_here, lon_count, channels = field_in.shape
    total_time = steps_here * lax.axis_size("tm")
    total_lat = rows_here * lax.axis_size("lat")
    time_base = lax.axis_index("tm") * steps_here
    lat_base = lax.axis_index("lat") * rows_here
    mask_local = window_mask(
        steps_here, rows_here, lon_count, time_base, lat_base, total_time, total_lat
    )
    local_fn = partial(local_shifted, allowed=mask_local)
    pair = shift_grid(jnp.stack((field_in, cotangent)), 1)
    pair = jnp.roll(pair, -(BWL // 2), axis=3)
    moved, grad_moved = pair[0], pair[1]
    middle, pull_local = jax.vjp(local_fn, moved, qkv_local, out_local)
    banded = middle.reshape(steps_here, 1, rows_here, lon_count, channels)
    grad_banded = grad_moved.reshape(steps_here, 1, rows_here, lon_count, channels)
    grad_grouped = lax.all_to_all(grad_banded, "lat", split_axis=3, concat_axis=1, tiled=True)
    grouped = lax.all_to_all(banded, "lat", split_axis=3, concat_axis=1, tiled=True)
    group_out, pull_dilated = jax.vjp(dilated_branch, grouped, qkv_dilated, out_dilated)
    grad_group_in, grad_qkv_d, grad_out_d = pull_dilated(grad_grouped)
    both_back = lax.all_to_all(
        jnp.stack((group_out, grad_group_in)), "lat", split_axis=2, concat_axis=4, tiled=True
    )
    total_mid = middle + both_back[0].reshape(middle.shape)
    grad_middle = grad_moved + both_back[1].reshape(middle.shape)
    grad_field_s, grad_qkv_s, grad_out_s = pull_local(grad_middle)
    factor = 1.0 / math.sqrt(total_time * total_lat * lon_count)
    parts = (grad_qkv_s * factor, grad_out_s * factor, grad_qkv_d * factor, grad_out_d * factor)
    results = jnp.roll(jnp.stack((total_mid, grad_field_s)), BWL // 2, axis=3)
    summed = butterfly_sum(parts, ("tm", "lat"), lambda: shift_grid(results, -1), 2)
    field_out, field_grad = summed[4][0], summed[4][1]
    return (field_out, field_grad, summed[0], summed[1], summed[2], summed[3])


def solution(mesh):
    return jax.shard_map(
        on_device,
        mesh=mesh,
        in_specs=(P("tm", "lat", None, None), P(), P(), P(), P(), P("tm", "lat", None, None)),
        out_specs=(P("tm", "lat", None, None), P("tm", "lat", None, None), P(), P(), P(), P()),
        check_vma=False,
    )
```

```python
from functools import partial
import math

import jax
import jax.numpy as jnp
from jax import lax
from jax.sharding import PartitionSpec as P

HEADS = 8
BT = 2
BH = 2
BWL = 16
BWD = 1


norm_eps = 1e-05


def from_behind(shard, axis, by):
    size = lax.axis_size(axis)
    return lax.ppermute(shard, axis, [(i, (i + by) % size) for i in range(size)])


def normalize(values):
    center = values - jnp.mean(values, axis=-1, keepdims=True)
    spread = jnp.mean(center * center, axis=-1, keepdims=True)
    return center * lax.rsqrt(spread + norm_eps)


def project(values, weight):
    flat = values.reshape(-1, values.shape[-1])
    result = jnp.dot(
        flat, weight, precision=lax.Precision.HIGHEST, preferred_element_type=jnp.float32
    )
    return result.reshape(values.shape[:-1] + (weight.shape[1],))


def to_windows(tensor):
    steps_n, rows_n, lons_n, feats_n = tensor.shape
    shaped = tensor.reshape(steps_n // BT, BT, rows_n // BH, BH, lons_n // BWL, BWL, feats_n)
    shaped = shaped.transpose(0, 2, 4, 1, 3, 5, 6)
    return shaped.reshape(steps_n // BT, rows_n // BH * (lons_n // BWL), BT * BH * BWL, feats_n)


def from_windows(windows, steps_n, rows_n, lons_n):
    feats_n = windows.shape[-1]
    shaped = windows.reshape(steps_n // BT, rows_n // BH, lons_n // BWL, BT, BH, BWL, feats_n)
    shaped = shaped.transpose(0, 3, 1, 4, 2, 5, 6)
    return shaped.reshape(steps_n, rows_n, lons_n, feats_n)


def to_groups(tensor):
    steps_n, bands_n, rows_n, lons_n, feats_n = tensor.shape
    shaped = tensor.reshape(steps_n, bands_n, rows_n, lons_n // BWD, BWD, feats_n)
    shaped = shaped.transpose(0, 2, 3, 1, 4, 5)
    return shaped.reshape(steps_n, rows_n * (lons_n // BWD), bands_n * BWD, feats_n)


def from_groups(groups, bands_n, rows_n, lons_n):
    steps_n = groups.shape[0]
    feats_n = groups.shape[-1]
    shaped = groups.reshape(steps_n, rows_n, lons_n // BWD, bands_n, BWD, feats_n)
    shaped = shaped.transpose(0, 3, 1, 2, 4, 5)
    return shaped.reshape(steps_n, bands_n, rows_n, lons_n, feats_n)


def window_mask(steps_n, rows_n, lons_n, time_base, lat_base, total_time, total_lat):
    time_pos = time_base + jnp.arange(steps_n, dtype=jnp.int32)
    lat_pos = lat_base + jnp.arange(rows_n, dtype=jnp.int32)
    time_flag = (time_pos >= total_time - BT // 2).astype(jnp.int32)
    lat_flag = (lat_pos >= total_lat - BH // 2).astype(jnp.int32)
    labels = (
        2 * time_flag[:, None, None]
        + lat_flag[None, :, None]
        + jnp.zeros((1, 1, lons_n), jnp.int32)
    )
    labelled = to_windows(labels[..., None])[..., 0]
    return labelled[..., :, None] == labelled[..., None, :]


def attend(packed, allowed):
    cells = packed.shape[1]
    channels = packed.shape[2] // 3
    head_dim = channels // HEADS
    queries = packed[..., :channels]
    keys_part = packed[..., channels:2 * channels]
    values_part = packed[..., 2 * channels:]
    head_of = (jnp.arange(channels) // head_dim)[:, None] == jnp.arange(HEADS)[None, :]
    head_of = head_of.astype(packed.dtype)
    spread_keys = jnp.swapaxes(keys_part, 1, 2)[:, :, None, :] * head_of[None, :, :, None]
    scores = jnp.einsum(
        "glc,gchm->glhm", queries, spread_keys, precision=lax.Precision.HIGHEST
    ) * head_dim ** (-0.5)
    exponent = jnp.exp(scores)
    if allowed is not None:
        exponent = jnp.where(allowed[:, :, None, :], exponent, 0.0)
    shares = exponent / jnp.sum(exponent, axis=-1, keepdims=True)
    spread_values = values_part[:, None, :, :] * jnp.transpose(head_of)[None, :, None, :]
    return jnp.einsum(
        "glhm,ghmc->glc", shares, spread_values, precision=lax.Precision.HIGHEST
    )


def dilated_branch(banded, weight_qkv, weight_out):
    mixed_qkv = project(normalize(banded), weight_qkv)
    groups = to_groups(mixed_qkv)
    cells = groups.shape[2]
    attended = attend(groups.reshape(-1, cells, groups.shape[3]), None)
    attended = attended.reshape(groups.shape[:3] + (banded.shape[4],))
    back = from_groups(attended, banded.shape[1], banded.shape[2], banded.shape[3])
    return project(back, weight_out)


def butterfly_stages(axes):
    stages = []
    for axis in axes:
        size = lax.axis_size(axis)
        bits = size.bit_length() - 1
        if size != 1 << bits:
            return None
        stages += [(axis, bit) for bit in range(bits)]
    return stages


def swap_partner(value, axis, bit):
    size = lax.axis_size(axis)
    return lax.ppermute(value, axis, [(i, i ^ (1 << bit)) for i in range(size)])


def butterfly_sum(parts, axes, side, side_stage, halvings=4):
    stages = butterfly_stages(axes)
    joined = jnp.concatenate(parts, axis=1)
    width = joined.shape[1]
    if stages is None or width % (128 << min(halvings, len(stages))):
        return lax.psum(parts, axes) + (side(),)
    halved = stages[:halvings]
    side_value = side()
    for index, (axis, bit) in enumerate(stages):
        if index == side_stage:
            side_value, joined = lax.optimization_barrier((side_value, joined))
        if index < len(halved):
            upper = (lax.axis_index(axis) >> bit) & 1
            half = joined.shape[1] // 2
            kept = lax.dynamic_slice_in_dim(joined, upper * half, half, axis=1)
            sent = lax.dynamic_slice_in_dim(joined, (1 - upper) * half, half, axis=1)
            joined = kept + swap_partner(sent, axis, bit)
        else:
            joined = joined + swap_partner(joined, axis, bit)
    for axis, bit in reversed(halved):
        upper = (lax.axis_index(axis) >> bit) & 1
        got = swap_partner(joined, axis, bit)
        joined = jnp.where(
            upper == 0,
            jnp.concatenate([joined, got], axis=1),
            jnp.concatenate([got, joined], axis=1),
        )
    out, start = [], 0
    for p in parts:
        out.append(joined[:, start:start + p.shape[1]])
        start += p.shape[1]
    return tuple(out) + (side_value,)


def shift_grid(stacked, step):
    time_edge = BT // 2
    lat_edge = BH // 2
    tm_size = lax.axis_size("tm")
    lat_size = lax.axis_size("lat")
    by = -step
    if step == 1:
        own = stacked[:, time_edge:, lat_edge:]
        lat_part = stacked[:, time_edge:, :lat_edge]
        tm_part = stacked[:, :time_edge, lat_edge:]
        corner = stacked[:, :time_edge, :lat_edge]
    else:
        own = stacked[:, :-time_edge, :-lat_edge]
        lat_part = stacked[:, :-time_edge, -lat_edge:]
        tm_part = stacked[:, -time_edge:, :-lat_edge]
        corner = stacked[:, -time_edge:, -lat_edge:]
    lat_part = from_behind(lat_part, "lat", by)
    tm_part = from_behind(tm_part, "tm", by)
    pairs = [
        (a * lat_size + b, ((a + by) % tm_size) * lat_size + (b + by) % lat_size)
        for a in range(tm_size)
        for b in range(lat_size)
    ]
    corner = lax.ppermute(corner, ("tm", "lat"), pairs)
    if step == 1:
        top = jnp.concatenate((own, lat_part), axis=2)
        bottom = jnp.concatenate((tm_part, corner), axis=2)
    else:
        top = jnp.concatenate((corner, tm_part), axis=2)
        bottom = jnp.concatenate((lat_part, own), axis=2)
    return jnp.concatenate((top, bottom), axis=1)


def local_shifted(moved, weight_qkv, weight_out, allowed):
    mixed_qkv = project(normalize(moved), weight_qkv)
    windows = to_windows(mixed_qkv)
    cells = windows.shape[2]
    attended = attend(
        windows.reshape(-1, cells, windows.shape[3]), allowed.reshape(-1, cells, cells)
    )
    attended = attended.reshape(windows.shape[:3] + (moved.shape[3],))
    back = from_windows(attended, moved.shape[0], moved.shape[1], moved.shape[2])
    return moved + project(back, weight_out)


def on_device(field_in, qkv_local, out_local, qkv_dilated, out_dilated, cotangent):
    steps_here, rows_here, lon_count, channels = field_in.shape
    total_time = steps_here * lax.axis_size("tm")
    total_lat = rows_here * lax.axis_size("lat")
    time_base = lax.axis_index("tm") * steps_here
    lat_base = lax.axis_index("lat") * rows_here
    mask_local = window_mask(
        steps_here, rows_here, lon_count, time_base, lat_base, total_time, total_lat
    )
    local_fn = partial(local_shifted, allowed=mask_local)
    pair = shift_grid(jnp.stack((field_in, cotangent)), 1)
    pair = jnp.roll(pair, -(BWL // 2), axis=3)
    moved, grad_moved = pair[0], pair[1]
    middle, pull_local = jax.vjp(local_fn, moved, qkv_local, out_local)
    banded = middle.reshape(steps_here, 1, rows_here, lon_count, channels)
    grad_banded = grad_moved.reshape(steps_here, 1, rows_here, lon_count, channels)
    both_out = lax.all_to_all(
        jnp.stack((banded, grad_banded)), "lat", split_axis=4, concat_axis=2, tiled=True
    )
    grouped, grad_grouped = both_out[0], both_out[1]
    group_out, pull_dilated = jax.vjp(dilated_branch, grouped, qkv_dilated, out_dilated)
    grad_group_in, grad_qkv_d, grad_out_d = pull_dilated(grad_grouped)
    both_back = lax.all_to_all(
        jnp.stack((group_out, grad_group_in)), "lat", split_axis=2, concat_axis=4, tiled=True
    )
    total_mid = middle + both_back[0].reshape(middle.shape)
    grad_middle = grad_moved + both_back[1].reshape(middle.shape)
    grad_field_s, grad_qkv_s, grad_out_s = pull_local(grad_middle)
    factor = 1.0 / math.sqrt(total_time * total_lat * lon_count)
    parts = (grad_qkv_s * factor, grad_out_s * factor, grad_qkv_d * factor, grad_out_d * factor)
    results = jnp.roll(jnp.stack((total_mid, grad_field_s)), BWL // 2, axis=3)
    summed = butterfly_sum(parts, ("tm", "lat"), lambda: shift_grid(results, -1), 2)
    field_out, field_grad = summed[4][0], summed[4][1]
    return (field_out, field_grad, summed[0], summed[1], summed[2], summed[3])


def solution(mesh):
    return jax.shard_map(
        on_device,
        mesh=mesh,
        in_specs=(P("tm", "lat", None, None), P(), P(), P(), P(), P("tm", "lat", None, None)),
        out_specs=(P("tm", "lat", None, None), P("tm", "lat", None, None), P(), P(), P(), P()),
        check_vma=False,
    )
```

```python
from functools import partial
import math

import jax
import jax.numpy as jnp
from jax import lax
from jax.sharding import PartitionSpec as P

HEADS = 8
BT = 2
BH = 2
BWL = 16
BWD = 1


norm_eps = 1e-05


def from_behind(shard, axis, by):
    size = lax.axis_size(axis)
    return lax.ppermute(shard, axis, [(i, (i + by) % size) for i in range(size)])


def normalize(values):
    center = values - jnp.mean(values, axis=-1, keepdims=True)
    spread = jnp.mean(center * center, axis=-1, keepdims=True)
    return center * lax.rsqrt(spread + norm_eps)


def project(values, weight):
    flat = values.reshape(-1, values.shape[-1])
    result = jnp.dot(
        flat, weight, precision=lax.Precision.HIGHEST, preferred_element_type=jnp.float32
    )
    return result.reshape(values.shape[:-1] + (weight.shape[1],))


def to_windows(tensor):
    steps_n, rows_n, lons_n, feats_n = tensor.shape
    shaped = tensor.reshape(steps_n // BT, BT, rows_n // BH, BH, lons_n // BWL, BWL, feats_n)
    shaped = shaped.transpose(0, 2, 4, 1, 3, 5, 6)
    return shaped.reshape(steps_n // BT, rows_n // BH * (lons_n // BWL), BT * BH * BWL, feats_n)


def from_windows(windows, steps_n, rows_n, lons_n):
    feats_n = windows.shape[-1]
    shaped = windows.reshape(steps_n // BT, rows_n // BH, lons_n // BWL, BT, BH, BWL, feats_n)
    shaped = shaped.transpose(0, 3, 1, 4, 2, 5, 6)
    return shaped.reshape(steps_n, rows_n, lons_n, feats_n)


def to_groups(tensor):
    steps_n, bands_n, rows_n, lons_n, feats_n = tensor.shape
    shaped = tensor.reshape(steps_n, bands_n, rows_n, lons_n // BWD, BWD, feats_n)
    shaped = shaped.transpose(0, 2, 3, 1, 4, 5)
    return shaped.reshape(steps_n, rows_n * (lons_n // BWD), bands_n * BWD, feats_n)


def from_groups(groups, bands_n, rows_n, lons_n):
    steps_n = groups.shape[0]
    feats_n = groups.shape[-1]
    shaped = groups.reshape(steps_n, rows_n, lons_n // BWD, bands_n, BWD, feats_n)
    shaped = shaped.transpose(0, 3, 1, 2, 4, 5)
    return shaped.reshape(steps_n, bands_n, rows_n, lons_n, feats_n)


def window_mask(steps_n, rows_n, lons_n, time_base, lat_base, total_time, total_lat):
    time_pos = time_base + jnp.arange(steps_n, dtype=jnp.int32)
    lat_pos = lat_base + jnp.arange(rows_n, dtype=jnp.int32)
    time_flag = (time_pos >= total_time - BT // 2).astype(jnp.int32)
    lat_flag = (lat_pos >= total_lat - BH // 2).astype(jnp.int32)
    labels = (
        2 * time_flag[:, None, None]
        + lat_flag[None, :, None]
        + jnp.zeros((1, 1, lons_n), jnp.int32)
    )
    labelled = to_windows(labels[..., None])[..., 0]
    return labelled[..., :, None] == labelled[..., None, :]


def attend(packed, allowed):
    cells = packed.shape[1]
    channels = packed.shape[2] // 3
    head_dim = channels // HEADS
    queries = packed[..., :channels]
    keys_part = packed[..., channels:2 * channels]
    values_part = packed[..., 2 * channels:]
    head_of = (jnp.arange(channels) // head_dim)[:, None] == jnp.arange(HEADS)[None, :]
    head_of = head_of.astype(packed.dtype)
    spread_keys = jnp.swapaxes(keys_part, 1, 2)[:, :, None, :] * head_of[None, :, :, None]
    scores = jnp.einsum(
        "glc,gchm->glhm", queries, spread_keys, precision=lax.Precision.HIGHEST
    ) * head_dim ** (-0.5)
    exponent = jnp.exp(scores)
    if allowed is not None:
        exponent = jnp.where(allowed[:, :, None, :], exponent, 0.0)
    shares = exponent / jnp.sum(exponent, axis=-1, keepdims=True)
    spread_values = values_part[:, None, :, :] * jnp.transpose(head_of)[None, :, None, :]
    return jnp.einsum(
        "glhm,ghmc->glc", shares, spread_values, precision=lax.Precision.HIGHEST
    )


def dilated_branch(banded, weight_qkv, weight_out):
    mixed_qkv = project(normalize(banded), weight_qkv)
    groups = to_groups(mixed_qkv)
    cells = groups.shape[2]
    attended = attend(groups.reshape(-1, cells, groups.shape[3]), None)
    attended = attended.reshape(groups.shape[:3] + (banded.shape[4],))
    back = from_groups(attended, banded.shape[1], banded.shape[2], banded.shape[3])
    return project(back, weight_out)


def butterfly_stages(axes):
    stages = []
    for axis in axes:
        size = lax.axis_size(axis)
        bits = size.bit_length() - 1
        if size != 1 << bits:
            return None
        stages += [(axis, bit) for bit in range(bits)]
    return stages


def swap_partner(value, axis, bit):
    size = lax.axis_size(axis)
    return lax.ppermute(value, axis, [(i, i ^ (1 << bit)) for i in range(size)])


def butterfly_sum(parts, axes, side, side_stage, halvings=4):
    stages = butterfly_stages(axes)
    joined = jnp.concatenate(parts, axis=1)
    width = joined.shape[1]
    if stages is None or width % (128 << min(halvings, len(stages))):
        return lax.psum(parts, axes) + (side(),)
    halved = stages[:halvings]
    side_value = side()
    for index, (axis, bit) in enumerate(stages):
        if index == side_stage:
            side_value, joined = lax.optimization_barrier((side_value, joined))
        if index < len(halved):
            upper = (lax.axis_index(axis) >> bit) & 1
            half = joined.shape[1] // 2
            kept = lax.dynamic_slice_in_dim(joined, upper * half, half, axis=1)
            sent = lax.dynamic_slice_in_dim(joined, (1 - upper) * half, half, axis=1)
            joined = kept + swap_partner(sent, axis, bit)
        else:
            joined = joined + swap_partner(joined, axis, bit)
    for axis, bit in reversed(halved):
        upper = (lax.axis_index(axis) >> bit) & 1
        got = swap_partner(joined, axis, bit)
        joined = jnp.where(
            upper == 0,
            jnp.concatenate([joined, got], axis=1),
            jnp.concatenate([got, joined], axis=1),
        )
    out, start = [], 0
    for p in parts:
        out.append(joined[:, start:start + p.shape[1]])
        start += p.shape[1]
    return tuple(out) + (side_value,)


def shift_grid(stacked, step):
    time_edge = BT // 2
    lat_edge = BH // 2
    tm_size = lax.axis_size("tm")
    lat_size = lax.axis_size("lat")
    by = -step
    if step == 1:
        own = stacked[:, time_edge:, lat_edge:]
        lat_part = stacked[:, time_edge:, :lat_edge]
        tm_part = stacked[:, :time_edge, lat_edge:]
        corner = stacked[:, :time_edge, :lat_edge]
    else:
        own = stacked[:, :-time_edge, :-lat_edge]
        lat_part = stacked[:, :-time_edge, -lat_edge:]
        tm_part = stacked[:, -time_edge:, :-lat_edge]
        corner = stacked[:, -time_edge:, -lat_edge:]
    lat_part = from_behind(lat_part, "lat", by)
    tm_part = from_behind(tm_part, "tm", by)
    pairs = [
        (a * lat_size + b, ((a + by) % tm_size) * lat_size + (b + by) % lat_size)
        for a in range(tm_size)
        for b in range(lat_size)
    ]
    corner = lax.ppermute(corner, ("tm", "lat"), pairs)
    if step == 1:
        top = jnp.concatenate((own, lat_part), axis=2)
        bottom = jnp.concatenate((tm_part, corner), axis=2)
    else:
        top = jnp.concatenate((corner, tm_part), axis=2)
        bottom = jnp.concatenate((lat_part, own), axis=2)
    return jnp.concatenate((top, bottom), axis=1)


def local_shifted(moved, weight_qkv, weight_out, allowed):
    mixed_qkv = project(normalize(moved), weight_qkv)
    windows = to_windows(mixed_qkv)
    cells = windows.shape[2]
    attended = attend(
        windows.reshape(-1, cells, windows.shape[3]), allowed.reshape(-1, cells, cells)
    )
    attended = attended.reshape(windows.shape[:3] + (moved.shape[3],))
    back = from_windows(attended, moved.shape[0], moved.shape[1], moved.shape[2])
    return moved + project(back, weight_out)


def on_device(field_in, qkv_local, out_local, qkv_dilated, out_dilated, cotangent):
    steps_here, rows_here, lon_count, channels = field_in.shape
    total_time = steps_here * lax.axis_size("tm")
    total_lat = rows_here * lax.axis_size("lat")
    time_base = lax.axis_index("tm") * steps_here
    lat_base = lax.axis_index("lat") * rows_here
    mask_local = window_mask(
        steps_here, rows_here, lon_count, time_base, lat_base, total_time, total_lat
    )
    local_fn = partial(local_shifted, allowed=mask_local)
    pair = shift_grid(jnp.stack((field_in, cotangent)), 1)
    pair = jnp.roll(pair, -(BWL // 2), axis=3)
    moved, grad_moved = pair[0], pair[1]
    middle, pull_local = jax.vjp(local_fn, moved, qkv_local, out_local)
    banded = middle.reshape(steps_here, 1, rows_here, lon_count, channels)
    grad_banded = grad_moved.reshape(steps_here, 1, rows_here, lon_count, channels)
    both_out = lax.all_to_all(
        jnp.stack((banded, grad_banded)), "lat", split_axis=4, concat_axis=2, tiled=True
    )
    grouped, grad_grouped = both_out[0], both_out[1]
    group_out, pull_dilated = jax.vjp(dilated_branch, grouped, qkv_dilated, out_dilated)
    grad_group_in, grad_qkv_d, grad_out_d = pull_dilated(grad_grouped)
    both_back = lax.all_to_all(
        jnp.stack((group_out, grad_group_in)), "lat", split_axis=2, concat_axis=4, tiled=True
    )
    total_mid = middle + both_back[0].reshape(middle.shape)
    grad_middle = grad_moved + both_back[1].reshape(middle.shape)
    grad_field_s, grad_qkv_s, grad_out_s = pull_local(grad_middle)
    factor = 1.0 / math.sqrt(total_time * total_lat * lon_count)
    parts = (grad_qkv_s * factor, grad_out_s * factor, grad_qkv_d * factor, grad_out_d * factor)
    results = jnp.roll(jnp.stack((total_mid, grad_field_s)), BWL // 2, axis=3)
    summed = butterfly_sum(parts, ("tm", "lat"), lambda: shift_grid(results, -1), 6)
    field_out, field_grad = summed[4][0], summed[4][1]
    return (field_out, field_grad, summed[0], summed[1], summed[2], summed[3])


def solution(mesh):
    return jax.shard_map(
        on_device,
        mesh=mesh,
        in_specs=(P("tm", "lat", None, None), P(), P(), P(), P(), P("tm", "lat", None, None)),
        out_specs=(P("tm", "lat", None, None), P("tm", "lat", None, None), P(), P(), P(), P()),
        check_vma=False,
    )
```

```python
from functools import partial
import math

import jax
import jax.numpy as jnp
from jax import lax
from jax.sharding import PartitionSpec as P

HEADS = 8
BT = 2
BH = 2
BWL = 16
BWD = 1


norm_eps = 1e-05


def from_behind(shard, axis, by):
    size = lax.axis_size(axis)
    return lax.ppermute(shard, axis, [(i, (i + by) % size) for i in range(size)])


def normalize(values):
    center = values - jnp.mean(values, axis=-1, keepdims=True)
    spread = jnp.mean(center * center, axis=-1, keepdims=True)
    return center * lax.rsqrt(spread + norm_eps)


def project(values, weight):
    flat = values.reshape(-1, values.shape[-1])
    result = jnp.dot(
        flat, weight, precision=lax.Precision.HIGHEST, preferred_element_type=jnp.float32
    )
    return result.reshape(values.shape[:-1] + (weight.shape[1],))


def to_windows(tensor):
    steps_n, rows_n, lons_n, feats_n = tensor.shape
    shaped = tensor.reshape(steps_n // BT, BT, rows_n // BH, BH, lons_n // BWL, BWL, feats_n)
    shaped = shaped.transpose(0, 2, 4, 1, 3, 5, 6)
    return shaped.reshape(steps_n // BT, rows_n // BH * (lons_n // BWL), BT * BH * BWL, feats_n)


def from_windows(windows, steps_n, rows_n, lons_n):
    feats_n = windows.shape[-1]
    shaped = windows.reshape(steps_n // BT, rows_n // BH, lons_n // BWL, BT, BH, BWL, feats_n)
    shaped = shaped.transpose(0, 3, 1, 4, 2, 5, 6)
    return shaped.reshape(steps_n, rows_n, lons_n, feats_n)


def to_groups(tensor):
    steps_n, bands_n, rows_n, lons_n, feats_n = tensor.shape
    shaped = tensor.reshape(steps_n, bands_n, rows_n, lons_n // BWD, BWD, feats_n)
    shaped = shaped.transpose(0, 2, 3, 1, 4, 5)
    return shaped.reshape(steps_n, rows_n * (lons_n // BWD), bands_n * BWD, feats_n)


def from_groups(groups, bands_n, rows_n, lons_n):
    steps_n = groups.shape[0]
    feats_n = groups.shape[-1]
    shaped = groups.reshape(steps_n, rows_n, lons_n // BWD, bands_n, BWD, feats_n)
    shaped = shaped.transpose(0, 3, 1, 2, 4, 5)
    return shaped.reshape(steps_n, bands_n, rows_n, lons_n, feats_n)


def window_mask(steps_n, rows_n, lons_n, time_base, lat_base, total_time, total_lat):
    time_pos = time_base + jnp.arange(steps_n, dtype=jnp.int32)
    lat_pos = lat_base + jnp.arange(rows_n, dtype=jnp.int32)
    time_flag = (time_pos >= total_time - BT // 2).astype(jnp.int32)
    lat_flag = (lat_pos >= total_lat - BH // 2).astype(jnp.int32)
    labels = (
        2 * time_flag[:, None, None]
        + lat_flag[None, :, None]
        + jnp.zeros((1, 1, lons_n), jnp.int32)
    )
    labelled = to_windows(labels[..., None])[..., 0]
    return labelled[..., :, None] == labelled[..., None, :]


def attend(packed, allowed):
    cells = packed.shape[1]
    channels = packed.shape[2] // 3
    head_dim = channels // HEADS
    queries = packed[..., :channels]
    keys_part = packed[..., channels:2 * channels]
    values_part = packed[..., 2 * channels:]
    head_of = (jnp.arange(channels) // head_dim)[:, None] == jnp.arange(HEADS)[None, :]
    head_of = head_of.astype(packed.dtype)
    spread_keys = jnp.swapaxes(keys_part, 1, 2)[:, :, None, :] * head_of[None, :, :, None]
    scores = jnp.einsum(
        "glc,gchm->glhm", queries, spread_keys, precision=lax.Precision.HIGHEST
    ) * head_dim ** (-0.5)
    exponent = jnp.exp(scores)
    if allowed is not None:
        exponent = jnp.where(allowed[:, :, None, :], exponent, 0.0)
    shares = exponent / jnp.sum(exponent, axis=-1, keepdims=True)
    spread_values = values_part[:, None, :, :] * jnp.transpose(head_of)[None, :, None, :]
    return jnp.einsum(
        "glhm,ghmc->glc", shares, spread_values, precision=lax.Precision.HIGHEST
    )


def dilated_branch(banded, weight_qkv, weight_out):
    mixed_qkv = project(normalize(banded), weight_qkv)
    groups = to_groups(mixed_qkv)
    cells = groups.shape[2]
    attended = attend(groups.reshape(-1, cells, groups.shape[3]), None)
    attended = attended.reshape(groups.shape[:3] + (banded.shape[4],))
    back = from_groups(attended, banded.shape[1], banded.shape[2], banded.shape[3])
    return project(back, weight_out)


def butterfly_stages(axes):
    stages = []
    for axis in axes:
        size = lax.axis_size(axis)
        bits = size.bit_length() - 1
        if size != 1 << bits:
            return None
        stages += [(axis, bit) for bit in range(bits)]
    return stages


def swap_partner(value, axis, bit):
    size = lax.axis_size(axis)
    return lax.ppermute(value, axis, [(i, i ^ (1 << bit)) for i in range(size)])


def butterfly_sum(parts, axes, side, side_stage, halvings=4):
    stages = butterfly_stages(axes)
    joined = jnp.concatenate(parts, axis=1)
    width = joined.shape[1]
    if stages is None or width % (128 << min(halvings, len(stages))):
        return lax.psum(parts, axes) + (side(),)
    halved = stages[:halvings]
    side_value = side()
    for index, (axis, bit) in enumerate(stages):
        if index == side_stage:
            side_value, joined = lax.optimization_barrier((side_value, joined))
        if index < len(halved):
            upper = (lax.axis_index(axis) >> bit) & 1
            half = joined.shape[1] // 2
            kept = lax.dynamic_slice_in_dim(joined, upper * half, half, axis=1)
            sent = lax.dynamic_slice_in_dim(joined, (1 - upper) * half, half, axis=1)
            joined = kept + swap_partner(sent, axis, bit)
        else:
            joined = joined + swap_partner(joined, axis, bit)
    for axis, bit in reversed(halved):
        upper = (lax.axis_index(axis) >> bit) & 1
        got = swap_partner(joined, axis, bit)
        joined = jnp.where(
            upper == 0,
            jnp.concatenate([joined, got], axis=1),
            jnp.concatenate([got, joined], axis=1),
        )
    out, start = [], 0
    for p in parts:
        out.append(joined[:, start:start + p.shape[1]])
        start += p.shape[1]
    return tuple(out) + (side_value,)


def shift_grid(stacked, step):
    time_edge = BT // 2
    lat_edge = BH // 2
    tm_size = lax.axis_size("tm")
    lat_size = lax.axis_size("lat")
    by = -step
    if step == 1:
        own = stacked[:, time_edge:, lat_edge:]
        lat_part = stacked[:, time_edge:, :lat_edge]
        tm_part = stacked[:, :time_edge, lat_edge:]
        corner = stacked[:, :time_edge, :lat_edge]
    else:
        own = stacked[:, :-time_edge, :-lat_edge]
        lat_part = stacked[:, :-time_edge, -lat_edge:]
        tm_part = stacked[:, -time_edge:, :-lat_edge]
        corner = stacked[:, -time_edge:, -lat_edge:]
    lat_part = from_behind(lat_part, "lat", by)
    tm_part = from_behind(tm_part, "tm", by)
    pairs = [
        (a * lat_size + b, ((a + by) % tm_size) * lat_size + (b + by) % lat_size)
        for a in range(tm_size)
        for b in range(lat_size)
    ]
    corner = lax.ppermute(corner, ("tm", "lat"), pairs)
    if step == 1:
        top = jnp.concatenate((own, lat_part), axis=2)
        bottom = jnp.concatenate((tm_part, corner), axis=2)
    else:
        top = jnp.concatenate((corner, tm_part), axis=2)
        bottom = jnp.concatenate((lat_part, own), axis=2)
    return jnp.concatenate((top, bottom), axis=1)


def local_shifted(moved, weight_qkv, weight_out, allowed):
    mixed_qkv = project(normalize(moved), weight_qkv)
    windows = to_windows(mixed_qkv)
    cells = windows.shape[2]
    attended = attend(
        windows.reshape(-1, cells, windows.shape[3]), allowed.reshape(-1, cells, cells)
    )
    attended = attended.reshape(windows.shape[:3] + (moved.shape[3],))
    back = from_windows(attended, moved.shape[0], moved.shape[1], moved.shape[2])
    return moved + project(back, weight_out)


def on_device(field_in, qkv_local, out_local, qkv_dilated, out_dilated, cotangent):
    steps_here, rows_here, lon_count, channels = field_in.shape
    total_time = steps_here * lax.axis_size("tm")
    total_lat = rows_here * lax.axis_size("lat")
    time_base = lax.axis_index("tm") * steps_here
    lat_base = lax.axis_index("lat") * rows_here
    mask_local = window_mask(
        steps_here, rows_here, lon_count, time_base, lat_base, total_time, total_lat
    )
    local_fn = partial(local_shifted, allowed=mask_local)
    pair = shift_grid(jnp.stack((field_in, cotangent)), 1)
    pair = jnp.roll(pair, -(BWL // 2), axis=3)
    moved, grad_moved = pair[0], pair[1]
    middle, pull_local = jax.vjp(local_fn, moved, qkv_local, out_local)
    banded = middle.reshape(steps_here, 1, rows_here, lon_count, channels)
    grad_banded = grad_moved.reshape(steps_here, 1, rows_here, lon_count, channels)
    both_out = lax.all_to_all(
        jnp.concatenate((banded, grad_banded), axis=-1), "lat", split_axis=3, concat_axis=1, tiled=True
    )
    grouped, grad_grouped = both_out[..., :channels], both_out[..., channels:]
    group_out, pull_dilated = jax.vjp(dilated_branch, grouped, qkv_dilated, out_dilated)
    grad_group_in, grad_qkv_d, grad_out_d = pull_dilated(grad_grouped)
    both_back = lax.all_to_all(
        jnp.concatenate((group_out, grad_group_in), axis=-1), "lat", split_axis=1, concat_axis=3, tiled=True
    )
    total_mid = middle + both_back[..., :channels].reshape(middle.shape)
    grad_middle = grad_moved + both_back[..., channels:].reshape(middle.shape)
    grad_field_s, grad_qkv_s, grad_out_s = pull_local(grad_middle)
    factor = 1.0 / math.sqrt(total_time * total_lat * lon_count)
    parts = (grad_qkv_s * factor, grad_out_s * factor, grad_qkv_d * factor, grad_out_d * factor)
    results = jnp.roll(jnp.stack((total_mid, grad_field_s)), BWL // 2, axis=3)
    summed = butterfly_sum(parts, ("tm", "lat"), lambda: shift_grid(results, -1), 6)
    field_out, field_grad = summed[4][0], summed[4][1]
    return (field_out, field_grad, summed[0], summed[1], summed[2], summed[3])


def solution(mesh):
    return jax.shard_map(
        on_device,
        mesh=mesh,
        in_specs=(P("tm", "lat", None, None), P(), P(), P(), P(), P("tm", "lat", None, None)),
        out_specs=(P("tm", "lat", None, None), P("tm", "lat", None, None), P(), P(), P(), P()),
        check_vma=False,
    )
```

```python
from functools import partial
import math

import jax
import jax.numpy as jnp
from jax import lax
from jax.sharding import PartitionSpec as P

HEADS = 8
BT = 2
BH = 2
BWL = 16
BWD = 1


norm_eps = 1e-05


def from_behind(shard, axis, by):
    size = lax.axis_size(axis)
    return lax.ppermute(shard, axis, [(i, (i + by) % size) for i in range(size)])


def normalize(values):
    center = values - jnp.mean(values, axis=-1, keepdims=True)
    spread = jnp.mean(center * center, axis=-1, keepdims=True)
    return center * lax.rsqrt(spread + norm_eps)


def project(values, weight):
    flat = values.reshape(-1, values.shape[-1])
    result = jnp.dot(
        flat, weight, precision=lax.Precision.HIGHEST, preferred_element_type=jnp.float32
    )
    return result.reshape(values.shape[:-1] + (weight.shape[1],))


def to_windows(tensor):
    steps_n, rows_n, lons_n, feats_n = tensor.shape
    shaped = tensor.reshape(steps_n // BT, BT, rows_n // BH, BH, lons_n // BWL, BWL, feats_n)
    shaped = shaped.transpose(0, 2, 4, 1, 3, 5, 6)
    return shaped.reshape(steps_n // BT, rows_n // BH * (lons_n // BWL), BT * BH * BWL, feats_n)


def from_windows(windows, steps_n, rows_n, lons_n):
    feats_n = windows.shape[-1]
    shaped = windows.reshape(steps_n // BT, rows_n // BH, lons_n // BWL, BT, BH, BWL, feats_n)
    shaped = shaped.transpose(0, 3, 1, 4, 2, 5, 6)
    return shaped.reshape(steps_n, rows_n, lons_n, feats_n)


def to_groups(tensor):
    steps_n, bands_n, rows_n, lons_n, feats_n = tensor.shape
    shaped = tensor.reshape(steps_n, bands_n, rows_n, lons_n // BWD, BWD, feats_n)
    shaped = shaped.transpose(0, 2, 3, 1, 4, 5)
    return shaped.reshape(steps_n, rows_n * (lons_n // BWD), bands_n * BWD, feats_n)


def from_groups(groups, bands_n, rows_n, lons_n):
    steps_n = groups.shape[0]
    feats_n = groups.shape[-1]
    shaped = groups.reshape(steps_n, rows_n, lons_n // BWD, bands_n, BWD, feats_n)
    shaped = shaped.transpose(0, 3, 1, 2, 4, 5)
    return shaped.reshape(steps_n, bands_n, rows_n, lons_n, feats_n)


def window_mask(steps_n, rows_n, lons_n, time_base, lat_base, total_time, total_lat):
    time_pos = time_base + jnp.arange(steps_n, dtype=jnp.int32)
    lat_pos = lat_base + jnp.arange(rows_n, dtype=jnp.int32)
    time_flag = (time_pos >= total_time - BT // 2).astype(jnp.int32)
    lat_flag = (lat_pos >= total_lat - BH // 2).astype(jnp.int32)
    labels = (
        2 * time_flag[:, None, None]
        + lat_flag[None, :, None]
        + jnp.zeros((1, 1, lons_n), jnp.int32)
    )
    labelled = to_windows(labels[..., None])[..., 0]
    return labelled[..., :, None] == labelled[..., None, :]


def attend(packed, allowed):
    cells = packed.shape[1]
    channels = packed.shape[2] // 3
    head_dim = channels // HEADS
    queries = packed[..., :channels]
    keys_part = packed[..., channels:2 * channels]
    values_part = packed[..., 2 * channels:]
    head_of = (jnp.arange(channels) // head_dim)[:, None] == jnp.arange(HEADS)[None, :]
    head_of = head_of.astype(packed.dtype)
    spread_keys = jnp.swapaxes(keys_part, 1, 2)[:, :, None, :] * head_of[None, :, :, None]
    scores = jnp.einsum(
        "glc,gchm->glhm", queries, spread_keys, precision=lax.Precision.HIGHEST
    ) * head_dim ** (-0.5)
    exponent = jnp.exp(scores)
    if allowed is not None:
        exponent = jnp.where(allowed[:, :, None, :], exponent, 0.0)
    shares = exponent / jnp.sum(exponent, axis=-1, keepdims=True)
    spread_values = values_part[:, None, :, :] * jnp.transpose(head_of)[None, :, None, :]
    return jnp.einsum(
        "glhm,ghmc->glc", shares, spread_values, precision=lax.Precision.HIGHEST
    )


def dilated_branch(banded, weight_qkv, weight_out):
    mixed_qkv = project(normalize(banded), weight_qkv)
    groups = to_groups(mixed_qkv)
    cells = groups.shape[2]
    attended = attend(groups.reshape(-1, cells, groups.shape[3]), None)
    attended = attended.reshape(groups.shape[:3] + (banded.shape[4],))
    back = from_groups(attended, banded.shape[1], banded.shape[2], banded.shape[3])
    return project(back, weight_out)


def butterfly_stages(axes):
    stages = []
    for axis in axes:
        size = lax.axis_size(axis)
        bits = size.bit_length() - 1
        if size != 1 << bits:
            return None
        order = list(range(bits))
        if bits >= 3:
            order = [0, 2, 1] + order[3:]
        stages += [(axis, bit) for bit in order]
    return stages


def swap_partner(value, axis, bit):
    size = lax.axis_size(axis)
    return lax.ppermute(value, axis, [(i, i ^ (1 << bit)) for i in range(size)])


def butterfly_sum(parts, axes, side, side_stage, halvings=4):
    stages = butterfly_stages(axes)
    joined = jnp.concatenate(parts, axis=1)
    width = joined.shape[1]
    if stages is None or width % (128 << min(halvings, len(stages))):
        return lax.psum(parts, axes) + (side(),)
    halved = stages[:halvings]
    side_value = side()
    for index, (axis, bit) in enumerate(stages):
        if index == side_stage:
            side_value, joined = lax.optimization_barrier((side_value, joined))
        if index < len(halved):
            upper = (lax.axis_index(axis) >> bit) & 1
            half = joined.shape[1] // 2
            kept = lax.dynamic_slice_in_dim(joined, upper * half, half, axis=1)
            sent = lax.dynamic_slice_in_dim(joined, (1 - upper) * half, half, axis=1)
            joined = kept + swap_partner(sent, axis, bit)
        else:
            joined = joined + swap_partner(joined, axis, bit)
    for axis, bit in reversed(halved):
        upper = (lax.axis_index(axis) >> bit) & 1
        got = swap_partner(joined, axis, bit)
        joined = jnp.where(
            upper == 0,
            jnp.concatenate([joined, got], axis=1),
            jnp.concatenate([got, joined], axis=1),
        )
    out, start = [], 0
    for p in parts:
        out.append(joined[:, start:start + p.shape[1]])
        start += p.shape[1]
    return tuple(out) + (side_value,)


def shift_grid(stacked, step):
    time_edge = BT // 2
    lat_edge = BH // 2
    tm_size = lax.axis_size("tm")
    lat_size = lax.axis_size("lat")
    by = -step
    if step == 1:
        own = stacked[:, time_edge:, lat_edge:]
        lat_part = stacked[:, time_edge:, :lat_edge]
        tm_part = stacked[:, :time_edge, lat_edge:]
        corner = stacked[:, :time_edge, :lat_edge]
    else:
        own = stacked[:, :-time_edge, :-lat_edge]
        lat_part = stacked[:, :-time_edge, -lat_edge:]
        tm_part = stacked[:, -time_edge:, :-lat_edge]
        corner = stacked[:, -time_edge:, -lat_edge:]
    lat_part = from_behind(lat_part, "lat", by)
    tm_part = from_behind(tm_part, "tm", by)
    pairs = [
        (a * lat_size + b, ((a + by) % tm_size) * lat_size + (b + by) % lat_size)
        for a in range(tm_size)
        for b in range(lat_size)
    ]
    corner = lax.ppermute(corner, ("tm", "lat"), pairs)
    if step == 1:
        top = jnp.concatenate((own, lat_part), axis=2)
        bottom = jnp.concatenate((tm_part, corner), axis=2)
    else:
        top = jnp.concatenate((corner, tm_part), axis=2)
        bottom = jnp.concatenate((lat_part, own), axis=2)
    return jnp.concatenate((top, bottom), axis=1)


def local_shifted(moved, weight_qkv, weight_out, allowed):
    mixed_qkv = project(normalize(moved), weight_qkv)
    windows = to_windows(mixed_qkv)
    cells = windows.shape[2]
    attended = attend(
        windows.reshape(-1, cells, windows.shape[3]), allowed.reshape(-1, cells, cells)
    )
    attended = attended.reshape(windows.shape[:3] + (moved.shape[3],))
    back = from_windows(attended, moved.shape[0], moved.shape[1], moved.shape[2])
    return moved + project(back, weight_out)


def on_device(field_in, qkv_local, out_local, qkv_dilated, out_dilated, cotangent):
    steps_here, rows_here, lon_count, channels = field_in.shape
    total_time = steps_here * lax.axis_size("tm")
    total_lat = rows_here * lax.axis_size("lat")
    time_base = lax.axis_index("tm") * steps_here
    lat_base = lax.axis_index("lat") * rows_here
    mask_local = window_mask(
        steps_here, rows_here, lon_count, time_base, lat_base, total_time, total_lat
    )
    local_fn = partial(local_shifted, allowed=mask_local)
    pair = shift_grid(jnp.stack((field_in, cotangent)), 1)
    pair = jnp.roll(pair, -(BWL // 2), axis=3)
    moved, grad_moved = pair[0], pair[1]
    middle, pull_local = jax.vjp(local_fn, moved, qkv_local, out_local)
    banded = middle.reshape(steps_here, 1, rows_here, lon_count, channels)
    grad_banded = grad_moved.reshape(steps_here, 1, rows_here, lon_count, channels)
    both_out = lax.all_to_all(
        jnp.concatenate((banded, grad_banded), axis=-1), "lat", split_axis=3, concat_axis=1, tiled=True
    )
    grouped, grad_grouped = both_out[..., :channels], both_out[..., channels:]
    group_out, pull_dilated = jax.vjp(dilated_branch, grouped, qkv_dilated, out_dilated)
    grad_group_in, grad_qkv_d, grad_out_d = pull_dilated(grad_grouped)
    both_back = lax.all_to_all(
        jnp.concatenate((group_out, grad_group_in), axis=-1), "lat", split_axis=1, concat_axis=3, tiled=True
    )
    total_mid = middle + both_back[..., :channels].reshape(middle.shape)
    grad_middle = grad_moved + both_back[..., channels:].reshape(middle.shape)
    grad_field_s, grad_qkv_s, grad_out_s = pull_local(grad_middle)
    factor = 1.0 / math.sqrt(total_time * total_lat * lon_count)
    parts = (grad_qkv_s * factor, grad_out_s * factor, grad_qkv_d * factor, grad_out_d * factor)
    results = jnp.roll(jnp.stack((total_mid, grad_field_s)), BWL // 2, axis=3)
    summed = butterfly_sum(parts, ("tm", "lat"), lambda: shift_grid(results, -1), 6)
    field_out, field_grad = summed[4][0], summed[4][1]
    return (field_out, field_grad, summed[0], summed[1], summed[2], summed[3])


def solution(mesh):
    return jax.shard_map(
        on_device,
        mesh=mesh,
        in_specs=(P("tm", "lat", None, None), P(), P(), P(), P(), P("tm", "lat", None, None)),
        out_specs=(P("tm", "lat", None, None), P("tm", "lat", None, None), P(), P(), P(), P()),
        check_vma=False,
    )
```

```python
from functools import partial
import math

import jax
import jax.numpy as jnp
from jax import lax
from jax.sharding import PartitionSpec as P

HEADS = 8
BT = 2
BH = 2
BWL = 16
BWD = 1


norm_eps = 1e-05


def from_behind(shard, axis, by):
    size = lax.axis_size(axis)
    return lax.ppermute(shard, axis, [(i, (i + by) % size) for i in range(size)])


def normalize(values):
    center = values - jnp.mean(values, axis=-1, keepdims=True)
    spread = jnp.mean(center * center, axis=-1, keepdims=True)
    return center * lax.rsqrt(spread + norm_eps)


def project(values, weight):
    flat = values.reshape(-1, values.shape[-1])
    result = jnp.dot(
        flat, weight, precision=lax.Precision.HIGHEST, preferred_element_type=jnp.float32
    )
    return result.reshape(values.shape[:-1] + (weight.shape[1],))


def to_windows(tensor):
    steps_n, rows_n, lons_n, feats_n = tensor.shape
    shaped = tensor.reshape(steps_n // BT, BT, rows_n // BH, BH, lons_n // BWL, BWL, feats_n)
    shaped = shaped.transpose(0, 2, 4, 1, 3, 5, 6)
    return shaped.reshape(steps_n // BT, rows_n // BH * (lons_n // BWL), BT * BH * BWL, feats_n)


def from_windows(windows, steps_n, rows_n, lons_n):
    feats_n = windows.shape[-1]
    shaped = windows.reshape(steps_n // BT, rows_n // BH, lons_n // BWL, BT, BH, BWL, feats_n)
    shaped = shaped.transpose(0, 3, 1, 4, 2, 5, 6)
    return shaped.reshape(steps_n, rows_n, lons_n, feats_n)


def to_groups(tensor):
    steps_n, bands_n, rows_n, lons_n, feats_n = tensor.shape
    shaped = tensor.reshape(steps_n, bands_n, rows_n, lons_n // BWD, BWD, feats_n)
    shaped = shaped.transpose(0, 2, 3, 1, 4, 5)
    return shaped.reshape(steps_n, rows_n * (lons_n // BWD), bands_n * BWD, feats_n)


def from_groups(groups, bands_n, rows_n, lons_n):
    steps_n = groups.shape[0]
    feats_n = groups.shape[-1]
    shaped = groups.reshape(steps_n, rows_n, lons_n // BWD, bands_n, BWD, feats_n)
    shaped = shaped.transpose(0, 3, 1, 2, 4, 5)
    return shaped.reshape(steps_n, bands_n, rows_n, lons_n, feats_n)


def window_mask(steps_n, rows_n, lons_n, time_base, lat_base, total_time, total_lat):
    time_pos = time_base + jnp.arange(steps_n, dtype=jnp.int32)
    lat_pos = lat_base + jnp.arange(rows_n, dtype=jnp.int32)
    time_flag = (time_pos >= total_time - BT // 2).astype(jnp.int32)
    lat_flag = (lat_pos >= total_lat - BH // 2).astype(jnp.int32)
    labels = (
        2 * time_flag[:, None, None]
        + lat_flag[None, :, None]
        + jnp.zeros((1, 1, lons_n), jnp.int32)
    )
    labelled = to_windows(labels[..., None])[..., 0]
    return labelled[..., :, None] == labelled[..., None, :]


def attend(packed, allowed):
    cells = packed.shape[1]
    channels = packed.shape[2] // 3
    head_dim = channels // HEADS
    queries = packed[..., :channels]
    keys_part = packed[..., channels:2 * channels]
    values_part = packed[..., 2 * channels:]
    head_of = (jnp.arange(channels) // head_dim)[:, None] == jnp.arange(HEADS)[None, :]
    head_of = head_of.astype(packed.dtype)
    spread_keys = jnp.swapaxes(keys_part, 1, 2)[:, :, None, :] * head_of[None, :, :, None]
    scores = jnp.einsum(
        "glc,gchm->glhm", queries, spread_keys, precision=lax.Precision.HIGHEST
    ) * head_dim ** (-0.5)
    exponent = jnp.exp(scores)
    if allowed is not None:
        exponent = jnp.where(allowed[:, :, None, :], exponent, 0.0)
    shares = exponent / jnp.sum(exponent, axis=-1, keepdims=True)
    spread_values = values_part[:, None, :, :] * jnp.transpose(head_of)[None, :, None, :]
    return jnp.einsum(
        "glhm,ghmc->glc", shares, spread_values, precision=lax.Precision.HIGHEST
    )


def dilated_branch(banded, weight_qkv, weight_out):
    mixed_qkv = project(normalize(banded), weight_qkv)
    groups = to_groups(mixed_qkv)
    cells = groups.shape[2]
    attended = attend(groups.reshape(-1, cells, groups.shape[3]), None)
    attended = attended.reshape(groups.shape[:3] + (banded.shape[4],))
    back = from_groups(attended, banded.shape[1], banded.shape[2], banded.shape[3])
    return project(back, weight_out)


def butterfly_stages(axes):
    stages = []
    for axis in axes:
        size = lax.axis_size(axis)
        bits = size.bit_length() - 1
        if size != 1 << bits:
            return None
        order = list(range(bits))
        if bits >= 3:
            order = [0, 2, 1] + order[3:]
        stages += [(axis, bit) for bit in order]
    return stages


def swap_partner(value, axis, bit):
    size = lax.axis_size(axis)
    return lax.ppermute(value, axis, [(i, i ^ (1 << bit)) for i in range(size)])


def butterfly_sum(parts, axes, side, side_stage, halvings=4):
    stages = butterfly_stages(axes)
    joined = jnp.concatenate(parts, axis=1)
    width = joined.shape[1]
    if stages is None or width % (128 << min(halvings, len(stages))):
        return lax.psum(parts, axes) + (side(),)
    halved = stages[:halvings]
    side_value = side()
    for index, (axis, bit) in enumerate(stages):
        if index == side_stage:
            side_value, joined = lax.optimization_barrier((side_value, joined))
        if index < len(halved):
            upper = (lax.axis_index(axis) >> bit) & 1
            half = joined.shape[1] // 2
            kept = lax.dynamic_slice_in_dim(joined, upper * half, half, axis=1)
            sent = lax.dynamic_slice_in_dim(joined, (1 - upper) * half, half, axis=1)
            joined = kept + swap_partner(sent, axis, bit)
        else:
            joined = joined + swap_partner(joined, axis, bit)
    for axis, bit in reversed(halved):
        upper = (lax.axis_index(axis) >> bit) & 1
        got = swap_partner(joined, axis, bit)
        joined = jnp.where(
            upper == 0,
            jnp.concatenate([joined, got], axis=1),
            jnp.concatenate([got, joined], axis=1),
        )
    out, start = [], 0
    for p in parts:
        out.append(joined[:, start:start + p.shape[1]])
        start += p.shape[1]
    return tuple(out) + (side_value,)


def shift_grid(stacked, step):
    time_edge = BT // 2
    lat_edge = BH // 2
    tm_size = lax.axis_size("tm")
    lat_size = lax.axis_size("lat")
    by = -step
    if step == 1:
        own = stacked[:, time_edge:, lat_edge:]
        lat_part = stacked[:, time_edge:, :lat_edge]
        tm_part = stacked[:, :time_edge, lat_edge:]
        corner = stacked[:, :time_edge, :lat_edge]
    else:
        own = stacked[:, :-time_edge, :-lat_edge]
        lat_part = stacked[:, :-time_edge, -lat_edge:]
        tm_part = stacked[:, -time_edge:, :-lat_edge]
        corner = stacked[:, -time_edge:, -lat_edge:]
    lat_part = from_behind(lat_part, "lat", by)
    tm_part = from_behind(tm_part, "tm", by)
    pairs = [
        (a * lat_size + b, ((a + by) % tm_size) * lat_size + (b + by) % lat_size)
        for a in range(tm_size)
        for b in range(lat_size)
    ]
    corner = lax.ppermute(corner, ("tm", "lat"), pairs)
    if step == 1:
        top = jnp.concatenate((own, lat_part), axis=2)
        bottom = jnp.concatenate((tm_part, corner), axis=2)
    else:
        top = jnp.concatenate((corner, tm_part), axis=2)
        bottom = jnp.concatenate((lat_part, own), axis=2)
    return jnp.concatenate((top, bottom), axis=1)


def local_shifted(moved, weight_qkv, weight_out, allowed):
    mixed_qkv = project(normalize(moved), weight_qkv)
    windows = to_windows(mixed_qkv)
    cells = windows.shape[2]
    attended = attend(
        windows.reshape(-1, cells, windows.shape[3]), allowed.reshape(-1, cells, cells)
    )
    attended = attended.reshape(windows.shape[:3] + (moved.shape[3],))
    back = from_windows(attended, moved.shape[0], moved.shape[1], moved.shape[2])
    return moved + project(back, weight_out)


def on_device(field_in, qkv_local, out_local, qkv_dilated, out_dilated, cotangent):
    steps_here, rows_here, lon_count, channels = field_in.shape
    total_time = steps_here * lax.axis_size("tm")
    total_lat = rows_here * lax.axis_size("lat")
    time_base = lax.axis_index("tm") * steps_here
    lat_base = lax.axis_index("lat") * rows_here
    mask_local = window_mask(
        steps_here, rows_here, lon_count, time_base, lat_base, total_time, total_lat
    )
    local_fn = partial(local_shifted, allowed=mask_local)
    pair = shift_grid(jnp.stack((field_in, cotangent)), 1)
    pair = jnp.roll(pair, -(BWL // 2), axis=3)
    moved, grad_moved = pair[0], pair[1]
    middle, pull_local = jax.vjp(local_fn, moved, qkv_local, out_local)
    banded = middle.reshape(steps_here, 1, rows_here, lon_count, channels)
    grad_banded = grad_moved.reshape(steps_here, 1, rows_here, lon_count, channels)
    both_out = lax.all_to_all(
        jnp.concatenate((banded, grad_banded), axis=-1), "lat", split_axis=3, concat_axis=1, tiled=True
    )
    grouped, grad_grouped = both_out[..., :channels], both_out[..., channels:]
    group_out, pull_dilated = jax.vjp(dilated_branch, grouped, qkv_dilated, out_dilated)
    grad_group_in, grad_qkv_d, grad_out_d = pull_dilated(grad_grouped)
    both_back = lax.all_to_all(
        jnp.concatenate((group_out, grad_group_in), axis=-1), "lat", split_axis=1, concat_axis=3, tiled=True
    )
    total_mid = middle + both_back[..., :channels].reshape(middle.shape)
    grad_middle = grad_moved + both_back[..., channels:].reshape(middle.shape)
    grad_field_s, grad_qkv_s, grad_out_s = pull_local(grad_middle)
    factor = 1.0 / math.sqrt(total_time * total_lat * lon_count)
    parts = (grad_qkv_s * factor, grad_out_s * factor, grad_qkv_d * factor, grad_out_d * factor)
    results = jnp.roll(jnp.stack((total_mid, grad_field_s)), BWL // 2, axis=3)
    summed = butterfly_sum(parts, ("tm", "lat"), lambda: shift_grid(results, -1), 7)
    field_out, field_grad = summed[4][0], summed[4][1]
    return (field_out, field_grad, summed[0], summed[1], summed[2], summed[3])


def solution(mesh):
    return jax.shard_map(
        on_device,
        mesh=mesh,
        in_specs=(P("tm", "lat", None, None), P(), P(), P(), P(), P("tm", "lat", None, None)),
        out_specs=(P("tm", "lat", None, None), P("tm", "lat", None, None), P(), P(), P(), P()),
        check_vma=False,
    )
```

```python
from functools import partial
import math

import jax
import jax.numpy as jnp
from jax import lax
from jax.sharding import PartitionSpec as P

HEADS = 8
BT = 2
BH = 2
BWL = 16
BWD = 1


norm_eps = 1e-05


def from_behind(shard, axis, by):
    size = lax.axis_size(axis)
    return lax.ppermute(shard, axis, [(i, (i + by) % size) for i in range(size)])


def normalize(values):
    center = values - jnp.mean(values, axis=-1, keepdims=True)
    spread = jnp.mean(center * center, axis=-1, keepdims=True)
    return center * lax.rsqrt(spread + norm_eps)


def project(values, weight):
    flat = values.reshape(-1, values.shape[-1])
    result = jnp.dot(
        flat, weight, precision=lax.Precision.HIGHEST, preferred_element_type=jnp.float32
    )
    return result.reshape(values.shape[:-1] + (weight.shape[1],))


def to_windows(tensor):
    steps_n, rows_n, lons_n, feats_n = tensor.shape
    shaped = tensor.reshape(steps_n // BT, BT, rows_n // BH, BH, lons_n // BWL, BWL, feats_n)
    shaped = shaped.transpose(0, 2, 4, 1, 3, 5, 6)
    return shaped.reshape(steps_n // BT, rows_n // BH * (lons_n // BWL), BT * BH * BWL, feats_n)


def from_windows(windows, steps_n, rows_n, lons_n):
    feats_n = windows.shape[-1]
    shaped = windows.reshape(steps_n // BT, rows_n // BH, lons_n // BWL, BT, BH, BWL, feats_n)
    shaped = shaped.transpose(0, 3, 1, 4, 2, 5, 6)
    return shaped.reshape(steps_n, rows_n, lons_n, feats_n)


def to_groups(tensor):
    steps_n, bands_n, rows_n, lons_n, feats_n = tensor.shape
    shaped = tensor.reshape(steps_n, bands_n, rows_n, lons_n // BWD, BWD, feats_n)
    shaped = shaped.transpose(0, 2, 3, 1, 4, 5)
    return shaped.reshape(steps_n, rows_n * (lons_n // BWD), bands_n * BWD, feats_n)


def from_groups(groups, bands_n, rows_n, lons_n):
    steps_n = groups.shape[0]
    feats_n = groups.shape[-1]
    shaped = groups.reshape(steps_n, rows_n, lons_n // BWD, bands_n, BWD, feats_n)
    shaped = shaped.transpose(0, 3, 1, 2, 4, 5)
    return shaped.reshape(steps_n, bands_n, rows_n, lons_n, feats_n)


def window_mask(steps_n, rows_n, lons_n, time_base, lat_base, total_time, total_lat):
    time_pos = time_base + jnp.arange(steps_n, dtype=jnp.int32)
    lat_pos = lat_base + jnp.arange(rows_n, dtype=jnp.int32)
    time_flag = (time_pos >= total_time - BT // 2).astype(jnp.int32)
    lat_flag = (lat_pos >= total_lat - BH // 2).astype(jnp.int32)
    labels = (
        2 * time_flag[:, None, None]
        + lat_flag[None, :, None]
        + jnp.zeros((1, 1, lons_n), jnp.int32)
    )
    labelled = to_windows(labels[..., None])[..., 0]
    return labelled[..., :, None] == labelled[..., None, :]


def attend(packed, allowed):
    cells = packed.shape[1]
    channels = packed.shape[2] // 3
    head_dim = channels // HEADS
    queries = packed[..., :channels]
    keys_part = packed[..., channels:2 * channels]
    values_part = packed[..., 2 * channels:]
    head_of = (jnp.arange(channels) // head_dim)[:, None] == jnp.arange(HEADS)[None, :]
    head_of = head_of.astype(packed.dtype)
    spread_keys = jnp.swapaxes(keys_part, 1, 2)[:, :, None, :] * head_of[None, :, :, None]
    scores = jnp.einsum(
        "glc,gchm->glhm", queries, spread_keys, precision=lax.Precision.HIGHEST
    ) * head_dim ** (-0.5)
    exponent = jnp.exp(scores)
    if allowed is not None:
        exponent = jnp.where(allowed[:, :, None, :], exponent, 0.0)
    shares = exponent / jnp.sum(exponent, axis=-1, keepdims=True)
    spread_values = values_part[:, None, :, :] * jnp.transpose(head_of)[None, :, None, :]
    return jnp.einsum(
        "glhm,ghmc->glc", shares, spread_values, precision=lax.Precision.HIGHEST
    )


def dilated_branch(banded, weight_qkv, weight_out):
    mixed_qkv = project(normalize(banded), weight_qkv)
    groups = to_groups(mixed_qkv)
    cells = groups.shape[2]
    attended = attend(groups.reshape(-1, cells, groups.shape[3]), None)
    attended = attended.reshape(groups.shape[:3] + (banded.shape[4],))
    back = from_groups(attended, banded.shape[1], banded.shape[2], banded.shape[3])
    return project(back, weight_out)


def butterfly_stages(axes):
    stages = []
    for axis in axes:
        size = lax.axis_size(axis)
        bits = size.bit_length() - 1
        if size != 1 << bits:
            return None
        order = list(range(bits))
        if bits >= 3:
            order = [0, 2, 1] + order[3:]
        stages += [(axis, bit) for bit in order]
    return stages


def swap_partner(value, axis, bit):
    size = lax.axis_size(axis)
    return lax.ppermute(value, axis, [(i, i ^ (1 << bit)) for i in range(size)])


def butterfly_sum(parts, axes, side, side_stage, halvings=4):
    stages = butterfly_stages(axes)
    joined = jnp.concatenate(parts, axis=1)
    width = joined.shape[1]
    if stages is None or width % (128 << min(halvings, len(stages))):
        return lax.psum(parts, axes) + (side(),)
    halved = stages[:halvings]
    side_value = side()
    for index, (axis, bit) in enumerate(stages):
        if index == side_stage:
            side_value, joined = lax.optimization_barrier((side_value, joined))
        if index < len(halved):
            upper = (lax.axis_index(axis) >> bit) & 1
            half = joined.shape[1] // 2
            kept = lax.dynamic_slice_in_dim(joined, upper * half, half, axis=1)
            sent = lax.dynamic_slice_in_dim(joined, (1 - upper) * half, half, axis=1)
            joined = kept + swap_partner(sent, axis, bit)
        else:
            joined = joined + swap_partner(joined, axis, bit)
    for axis, bit in reversed(halved):
        upper = (lax.axis_index(axis) >> bit) & 1
        got = swap_partner(joined, axis, bit)
        half = joined.shape[1]
        placed = jnp.zeros((joined.shape[0], 2 * half), joined.dtype)
        placed = lax.dynamic_update_slice_in_dim(placed, joined, upper * half, axis=1)
        joined = lax.dynamic_update_slice_in_dim(placed, got, (1 - upper) * half, axis=1)
    out, start = [], 0
    for p in parts:
        out.append(joined[:, start:start + p.shape[1]])
        start += p.shape[1]
    return tuple(out) + (side_value,)


def shift_grid(stacked, step):
    time_edge = BT // 2
    lat_edge = BH // 2
    tm_size = lax.axis_size("tm")
    lat_size = lax.axis_size("lat")
    by = -step
    if step == 1:
        own = stacked[:, time_edge:, lat_edge:]
        lat_part = stacked[:, time_edge:, :lat_edge]
        tm_part = stacked[:, :time_edge, lat_edge:]
        corner = stacked[:, :time_edge, :lat_edge]
    else:
        own = stacked[:, :-time_edge, :-lat_edge]
        lat_part = stacked[:, :-time_edge, -lat_edge:]
        tm_part = stacked[:, -time_edge:, :-lat_edge]
        corner = stacked[:, -time_edge:, -lat_edge:]
    lat_part = from_behind(lat_part, "lat", by)
    tm_part = from_behind(tm_part, "tm", by)
    pairs = [
        (a * lat_size + b, ((a + by) % tm_size) * lat_size + (b + by) % lat_size)
        for a in range(tm_size)
        for b in range(lat_size)
    ]
    corner = lax.ppermute(corner, ("tm", "lat"), pairs)
    if step == 1:
        top = jnp.concatenate((own, lat_part), axis=2)
        bottom = jnp.concatenate((tm_part, corner), axis=2)
    else:
        top = jnp.concatenate((corner, tm_part), axis=2)
        bottom = jnp.concatenate((lat_part, own), axis=2)
    return jnp.concatenate((top, bottom), axis=1)


def local_shifted(moved, weight_qkv, weight_out, allowed):
    mixed_qkv = project(normalize(moved), weight_qkv)
    windows = to_windows(mixed_qkv)
    cells = windows.shape[2]
    attended = attend(
        windows.reshape(-1, cells, windows.shape[3]), allowed.reshape(-1, cells, cells)
    )
    attended = attended.reshape(windows.shape[:3] + (moved.shape[3],))
    back = from_windows(attended, moved.shape[0], moved.shape[1], moved.shape[2])
    return moved + project(back, weight_out)


def on_device(field_in, qkv_local, out_local, qkv_dilated, out_dilated, cotangent):
    steps_here, rows_here, lon_count, channels = field_in.shape
    total_time = steps_here * lax.axis_size("tm")
    total_lat = rows_here * lax.axis_size("lat")
    time_base = lax.axis_index("tm") * steps_here
    lat_base = lax.axis_index("lat") * rows_here
    mask_local = window_mask(
        steps_here, rows_here, lon_count, time_base, lat_base, total_time, total_lat
    )
    local_fn = partial(local_shifted, allowed=mask_local)
    pair = shift_grid(jnp.stack((field_in, cotangent)), 1)
    pair = jnp.roll(pair, -(BWL // 2), axis=3)
    moved, grad_moved = pair[0], pair[1]
    middle, pull_local = jax.vjp(local_fn, moved, qkv_local, out_local)
    banded = middle.reshape(steps_here, 1, rows_here, lon_count, channels)
    grad_banded = grad_moved.reshape(steps_here, 1, rows_here, lon_count, channels)
    both_out = lax.all_to_all(
        jnp.concatenate((banded, grad_banded), axis=-1), "lat", split_axis=3, concat_axis=1, tiled=True
    )
    grouped, grad_grouped = both_out[..., :channels], both_out[..., channels:]
    group_out, pull_dilated = jax.vjp(dilated_branch, grouped, qkv_dilated, out_dilated)
    grad_group_in, grad_qkv_d, grad_out_d = pull_dilated(grad_grouped)
    both_back = lax.all_to_all(
        jnp.concatenate((group_out, grad_group_in), axis=-1), "lat", split_axis=1, concat_axis=3, tiled=True
    )
    total_mid = middle + both_back[..., :channels].reshape(middle.shape)
    grad_middle = grad_moved + both_back[..., channels:].reshape(middle.shape)
    grad_field_s, grad_qkv_s, grad_out_s = pull_local(grad_middle)
    factor = 1.0 / math.sqrt(total_time * total_lat * lon_count)
    parts = (grad_qkv_s * factor, grad_out_s * factor, grad_qkv_d * factor, grad_out_d * factor)
    results = jnp.roll(jnp.stack((total_mid, grad_field_s)), BWL // 2, axis=3)
    summed = butterfly_sum(parts, ("tm", "lat"), lambda: shift_grid(results, -1), 6)
    field_out, field_grad = summed[4][0], summed[4][1]
    return (field_out, field_grad, summed[0], summed[1], summed[2], summed[3])


def solution(mesh):
    return jax.shard_map(
        on_device,
        mesh=mesh,
        in_specs=(P("tm", "lat", None, None), P(), P(), P(), P(), P("tm", "lat", None, None)),
        out_specs=(P("tm", "lat", None, None), P("tm", "lat", None, None), P(), P(), P(), P()),
        check_vma=False,
    )
```
